256 devices in a mesh: chan: 16 (over z, core), tm: 16 (over x, y).
Axes of the slice: x: 4, y: 4, z: 8, core: 2. Of those that a mesh axis runs over, the one named last changes fastest.
Arguments:
- signal: bfloat16 [512, 131072], P('chan', 'tm'), may hold values from -6 to 6
- pair_band: int32 [16, 512, 8], P('tm', 'chan'), may hold values from 0 to 255, as said below
- pair_offset: int32 [16, 512, 8], P('tm', 'chan'), may hold values from 1 to 8
- pair_owner: int32 [16, 512, 8, 1], P('tm', 'chan'), may hold values from 0 to 15; in each aligned block of 256 rows (0 to 255, 256 to 511, ..., all dimensions but the last counted through in order) at most 48 rows name the same one
Outputs:
- cyclic_map: bfloat16 [16, 16, 16, 48, 2048], P('tm', 'chan')
The draws below stay inside these ranges and needn't reach their ends.
Inputs may be any that keep to these rules, and one draw needn't show every extreme that they name: `pair_band`: entry [t, c, q] is a band of the t-th block, t * 16 to (t + 1) * 16 - 1. `pair_owner`: among the 256 rows of one device (one block of bands, one channel group) no owner appears more than 48 times, and in some devices one owner appears exactly 48 times.
All inputs are finite; a program needn't handle non-finite values.
Results may differ from the reference program's by a relative error of at most 0.0079.
Values may be sent and summed in bfloat16 or wider, within the bound.
No kernel may reach another device: no remote copies, remote signals or barrier semaphores. Data moves between devices by JAX's collectives and lax.ppermute only.
A program may use at most 128 MiB of HBM per device.

```python
import math
import jax
import jax.numpy as jnp
import numpy as np
from jax import lax

BANDS = 256
HOP = 64
FRAMES = 2048
KEEP = 1024
DMAX = 8
CH_GROUP = 32
PAIRS = 8
BLOCKS = 16
GROUPS = 16
CHANNELS = 512
SAMPLES = 131072
BAND_DEV = 16
CAP = 48


def draw_pair_band(key, part):
    within = jax.random.randint(key, (BLOCKS, CHANNELS, PAIRS), 0, BAND_DEV).astype(jnp.int32)
    start = jnp.arange(BLOCKS, dtype=jnp.int32)[:, None, None] * BAND_DEV
    bands = within + start
    bands = bands.at[0, 0, 0].set(0)
    bands = bands.at[BLOCKS - 1, 0, 0].set(BANDS - 1)
    return bands.astype(jnp.int32)


def place_ends(result, rng, least, high):
    index_at = [jax.random.randint(jax.random.fold_in(rng, axis), (), 0, length) for axis, length in enumerate(result.shape)]
    widest = result.shape.index(max(result.shape))
    beside = index_at[:widest] + [(index_at[widest] + 1) % result.shape[widest]] + index_at[widest + 1:]
    return result.at[tuple(index_at)].set(least).at[tuple(beside)].set(high)


def steps_of(own_key, shape, shards, least, high):
    gain = 1.0
    for position, parts in shards:
        steps = jax.random.uniform(jax.random.fold_in(jax.random.fold_in(own_key, 6), position), (parts,), jnp.float32, least / len(shards), high / len(shards))
        gain = gain * jnp.repeat(jnp.exp(steps), shape[position] // parts).reshape((-1,) + (1,) * (len(shape) - 1 - position))
    return gain


def deal_out(stream_key, own, number, rows, amount, top, reach, slope):
    order = jax.random.permutation(stream_key, amount)
    heavy_load, usual = load_shares(amount, rows * top, reach, slope, True), load_shares(amount, rows * top, reach, slope, False)
    places = jnp.arange(amount)

    def named(lengths, offset_by):
        used = int((lengths > 0).sum())
        fixed = max(1, used // 4)
        shifted = fixed + (places - fixed + offset_by * (used - fixed)) % max(1, amount - fixed)
        return jnp.zeros((amount,), jnp.int32).at[order[jnp.where(places < fixed, places, shifted)]].set(jnp.asarray(lengths, jnp.int32))

    lengths = jnp.where(number % 4 == 0, named(heavy_load, number // 4), named(usual, number - number // 4 - 1))
    mixed = jax.random.permutation(jax.random.fold_in(own, 3), amount)
    donor, sink = mixed[0:amount // 2 * 2:2], mixed[1:amount // 2 * 2:2]
    slack = jnp.minimum(lengths[donor] - 1, reach - lengths[sink]) // 2
    slack = jnp.where((donor == order[0]) | (sink == order[0]) | (lengths[sink] == 0), 0, jnp.maximum(slack, 0))
    shifted = jax.random.randint(jax.random.fold_in(own, 4), (amount // 2,), 0, 1 << 20) % (slack + 1)
    lengths = lengths.at[donor].add(-shifted).at[sink].add(shifted)
    items = jnp.searchsorted(jnp.cumsum(lengths), jnp.arange(rows * top), side="right").astype(jnp.int32)
    grid = items.reshape(top, rows).T
    grid = grid[jax.random.permutation(jax.random.fold_in(own, 1), rows)]
    offset_by = jax.random.randint(jax.random.fold_in(own, 2), (rows, 1), 0, top)
    return jnp.take_along_axis(grid, (jnp.arange(top)[None, :] + offset_by) % top, axis=1)


def load_shares(amount, total, reach, lean, full):
    loads = [(1 << 20) // math.isqrt(grade ** lean) + 1 for grade in range(1, amount + 1)]
    largest = reach if full else min(reach, max(-(-total // amount), total * loads[0] // sum(loads)))
    least = 1 if total - largest >= amount - 1 else 0
    given, rest = [largest] + [least] * (amount - 1), total - largest - least * (amount - 1)
    while rest > 0:
        candidates = [i for i in range(1, amount) if given[i] < largest] or [i for i in range(1, amount) if given[i] < reach]
        pool, budget = sum([loads[i] for i in candidates]), rest
        for i in candidates:
            more = min(reach - given[i], max(1, budget * loads[i] // pool), rest)
            given[i] = given[i] + more
            rest = rest - more
    return np.array(given)


def normal_values(rng, dims, width, limit, cuts=(), kind=jnp.bfloat16):
    drawn = jax.random.normal(rng, dims, jnp.float32) * width
    if len(cuts) > 0:
        drawn = steps_of(rng, dims, cuts, -0.22, 0.18) * drawn
    return jnp.clip(drawn, min=-limit, max=limit).astype(kind)


def setup_inputs(seed: int = 0) -> dict:
    key_list = jax.random.split(jax.random.key(seed), 5)
    signal = normal_values(key_list[0], (CHANNELS, SAMPLES), 1.0, 6.0, ((0, 16), (1, 16)))
    pair_band = draw_pair_band(jax.random.fold_in(key_list[4], 71), 0)
    pair_offset = place_ends(jax.random.randint(key_list[2], (BLOCKS, CHANNELS, PAIRS), 1, DMAX + 1), jax.random.fold_in(key_list[2], 1), 1, DMAX).astype(jnp.int32)
    pair_owner_keys = jax.random.split(jax.random.fold_in(key_list[3], 1), BLOCKS * CHANNELS * PAIRS // (CH_GROUP * PAIRS))
    pair_owner_turns = jax.random.permutation(jax.random.fold_in(key_list[3], 3), BLOCKS * CHANNELS * PAIRS // (CH_GROUP * PAIRS))
    pair_owner = jax.vmap(lambda own, number: deal_out(jax.random.fold_in(key_list[3], 2), own, number, CH_GROUP * PAIRS, GROUPS, 1, CAP, 2))(pair_owner_keys, pair_owner_turns).reshape((BLOCKS, CHANNELS, PAIRS, 1))
    return {"signal": signal, "pair_band": pair_band, "pair_offset": pair_offset, "pair_owner": pair_owner}


def bank_matrix(bands):
    index = jnp.arange(bands, dtype=jnp.int32)
    angle = (index[:, None] * index[None, :] % bands).astype(jnp.float32) * (2.0 * math.pi / bands)
    window = 0.5 - 0.5 * jnp.cos((index.astype(jnp.float32) + 0.5) * (2.0 * math.pi / bands))
    scaled = window / math.sqrt(3.0 * bands / 8.0)
    return jnp.concatenate([scaled[:, None] * jnp.cos(angle), -scaled[:, None] * jnp.sin(angle)], axis=1).astype(jnp.bfloat16)

def fourier_block(start, count, frames, keep):
    moment = start + jnp.arange(count, dtype=jnp.int32)
    cycles = jnp.arange(keep, dtype=jnp.int32)
    angle = (moment[:, None] * cycles[None, :] % frames).astype(jnp.float32) * (2.0 * math.pi / frames)
    cosine = jnp.cos(angle) / math.sqrt(frames)
    sine = jnp.sin(angle) / math.sqrt(frames)
    upper_half = jnp.concatenate([cosine, -sine], axis=1)
    lower_half = jnp.concatenate([sine, cosine], axis=1)
    return jnp.concatenate([upper_half, lower_half], axis=0).astype(jnp.bfloat16)

def demodulate(first, second, offset):
    real_part = first[..., 0, :] * second[..., 0, :] + first[..., 1, :] * second[..., 1, :]
    imag_part = first[..., 1, :] * second[..., 0, :] - first[..., 0, :] * second[..., 1, :]
    shift_bins = (offset * (HOP * FRAMES // BANDS) - KEEP // 2) % FRAMES
    moment = jnp.arange(FRAMES, dtype=jnp.int32)
    angle = (shift_bins[..., None] * moment % FRAMES).astype(jnp.float32) * (2.0 * math.pi / FRAMES)
    cosine = jnp.cos(angle)
    sine = jnp.sin(angle)
    return jnp.concatenate([real_part * cosine + imag_part * sine, imag_part * cosine - real_part * sine], axis=-1).astype(jnp.bfloat16)

def reference(signal, pair_band, pair_offset, pair_owner):
    bank_table = bank_matrix(BANDS)
    dft_table = fourier_block(0, FRAMES, FRAMES, KEEP)
    stride_count = BANDS // HOP
    row_count = CH_GROUP * PAIRS
    records_all = signal.reshape(GROUPS, CH_GROUP, SAMPLES)
    bands_all = pair_band.reshape(BLOCKS, GROUPS, CH_GROUP, PAIRS).transpose(1, 0, 2, 3)
    offsets_all = pair_offset.reshape(BLOCKS, GROUPS, CH_GROUP, PAIRS).transpose(1, 0, 2, 3)
    owners_all = pair_owner.reshape(BLOCKS, GROUPS, row_count).transpose(1, 0, 2)

    def one_group(inputs):
        records, band_group, offset_group, owner_group = inputs
        padded = jnp.pad(records, ((0, 0), (0, BANDS - HOP)))
        pieces = padded.reshape(CH_GROUP, FRAMES + stride_count - 1, HOP)
        framed = jnp.concatenate([pieces[:, part_index:part_index + FRAMES, :] for part_index in range(stride_count)], axis=2)
        spectra = jnp.einsum('cmn,nk->ckm', framed.astype(jnp.float32), bank_table.astype(jnp.float32)).astype(jnp.bfloat16)
        spectra = spectra.reshape(CH_GROUP, 2, BANDS, FRAMES)
        spectra = jnp.pad(spectra, ((0, 0), (0, 0), (0, DMAX), (0, 0)))
        channel_index = jnp.arange(CH_GROUP, dtype=jnp.int32)[None, :, None]
        first = spectra[channel_index, :, band_group].astype(jnp.float32)
        second = spectra[channel_index, :, band_group + offset_group].astype(jnp.float32)
        demod = demodulate(first, second, offset_group).reshape(BLOCKS, row_count, 2 * FRAMES)
        correlation = jnp.einsum('trj,jk->trk', demod.astype(jnp.float32), dft_table.astype(jnp.float32)).astype(jnp.bfloat16)
        hits = (owner_group[..., None] == jnp.arange(GROUPS, dtype=jnp.int32)).astype(jnp.int32)
        rank = lax.optimization_barrier(jnp.sum((jnp.cumsum(hits, axis=1) - 1) * hits, axis=2))
        slot = owner_group * CAP + rank
        block_index = jnp.arange(BLOCKS, dtype=jnp.int32)[:, None]
        placed = jnp.zeros((BLOCKS, GROUPS * CAP, 2 * KEEP), jnp.bfloat16).at[block_index, slot].set(correlation)
        return placed.reshape(BLOCKS, GROUPS, CAP, 2 * KEEP)
    maps = lax.map(one_group, (records_all, bands_all, offsets_all, owners_all))
    return maps.transpose(1, 2, 0, 3, 4)
```

```python
import math

import jax
import jax.numpy as jnp
from jax import lax
from jax.sharding import PartitionSpec as P

BANDS = 256
HOP = 64
FRAMES = 2048
KEEP = 1024
DMAX = 8


def passed_along(array, axis, by):
    devices = lax.axis_size(axis)
    pairs = [(i, i + by) for i in range(devices) if 0 <= i + by < devices]
    return lax.ppermute(array, axis, pairs)


def bank_matrix(bands):
    index = jnp.arange(bands, dtype=jnp.int32)
    angle = (index[:, None] * index[None, :] % bands).astype(jnp.float32) * (2.0 * math.pi / bands)
    window = 0.5 - 0.5 * jnp.cos((index.astype(jnp.float32) + 0.5) * (2.0 * math.pi / bands))
    scaled = window / math.sqrt(3.0 * bands / 8.0)
    return jnp.concatenate(
        [scaled[:, None] * jnp.cos(angle), -scaled[:, None] * jnp.sin(angle)], axis=1
    ).astype(jnp.bfloat16)


def turn_table(moments, cycles):
    angle = (moments[:, None] * cycles[None, :] % FRAMES).astype(jnp.float32) * (
        2.0 * math.pi / FRAMES
    )
    return jnp.cos(angle), jnp.sin(angle)


def fourier_tables():
    cycles = jnp.arange(KEEP, dtype=jnp.int32)
    coarse_cos, coarse_sin = turn_table(32 * jnp.arange(FRAMES // 32, dtype=jnp.int32), cycles)
    fine_cos, fine_sin = turn_table(jnp.arange(32, dtype=jnp.int32), cycles)
    scale = 1.0 / math.sqrt(FRAMES)
    cosine = (
        coarse_cos[:, None, :] * fine_cos[None, :, :] - coarse_sin[:, None, :] * fine_sin[None, :, :]
    ) * scale
    sine = (
        coarse_sin[:, None, :] * fine_cos[None, :, :] + coarse_cos[:, None, :] * fine_sin[None, :, :]
    ) * scale
    return (
        cosine.reshape(FRAMES, KEEP).astype(jnp.bfloat16),
        sine.reshape(FRAMES, KEEP).astype(jnp.bfloat16),
    )


def on_device(signal, pair_band, pair_offset, pair_owner):
    channels = signal.shape[0]
    stride_count = BANDS // HOP
    frames_dev = signal.shape[1] // HOP
    blocks = lax.axis_size("tm")
    bank_table = bank_matrix(BANDS)
    sample_tail = passed_along(signal[:, : BANDS - HOP], "tm", -1)
    records = jnp.concatenate([signal, sample_tail], axis=1)
    pieces = records.reshape(channels, frames_dev + stride_count - 1, HOP)
    framed = jnp.concatenate(
        [pieces[:, part_index : part_index + frames_dev, :] for part_index in range(stride_count)],
        axis=2,
    )
    spectra = jnp.einsum(
        "cmn,nk->ckm", framed, bank_table, preferred_element_type=jnp.float32
    ).astype(jnp.bfloat16)
    spectra = spectra.reshape(channels, 2, BANDS, frames_dev)

    bands_all = lax.all_gather(pair_band[0], "tm", axis=1, tiled=False)
    offsets_all = lax.all_gather(pair_offset[0], "tm", axis=1, tiled=False)
    pairs = bands_all.shape[2]
    band_first = bands_all.reshape(channels, blocks * pairs)
    offset = offsets_all.reshape(channels, blocks * pairs)
    positions = jnp.arange(BANDS, dtype=jnp.int32)
    pick_first = (band_first[..., None] == positions).astype(jnp.bfloat16)
    pick_second = ((band_first + offset)[..., None] == positions).astype(jnp.bfloat16)
    first = jnp.einsum("crb,cpbm->crpm", pick_first, spectra, preferred_element_type=jnp.float32)
    second = jnp.einsum("crb,cpbm->crpm", pick_second, spectra, preferred_element_type=jnp.float32)
    real_part = first[:, :, 0] * second[:, :, 0] + first[:, :, 1] * second[:, :, 1]
    imag_part = first[:, :, 1] * second[:, :, 0] - first[:, :, 0] * second[:, :, 1]

    moment = lax.axis_index("tm") * frames_dev + jnp.arange(frames_dev, dtype=jnp.int32)
    shift_bins = (jnp.arange(1, DMAX + 1, dtype=jnp.int32) * (HOP * FRAMES // BANDS) - KEEP // 2) % FRAMES
    phase_cos, phase_sin = turn_table(shift_bins, moment)
    cosine = jnp.zeros(offset.shape + (frames_dev,), jnp.float32)
    sine = jnp.zeros(offset.shape + (frames_dev,), jnp.float32)
    for index in range(DMAX):
        chosen = (offset == index + 1)[..., None]
        cosine = jnp.where(chosen, phase_cos[index], cosine)
        sine = jnp.where(chosen, phase_sin[index], sine)
    demod_re = (real_part * cosine + imag_part * sine).astype(jnp.bfloat16)
    demod_im = (imag_part * cosine - real_part * sine).astype(jnp.bfloat16)
    demod = jnp.stack([demod_re, demod_im], axis=0)
    demod = demod.reshape(2, channels, blocks, pairs, frames_dev).transpose(0, 1, 3, 2, 4)
    arrived = lax.all_to_all(demod, "tm", split_axis=3, concat_axis=3, tiled=True)
    rows = channels * pairs
    arrived = arrived.reshape(2 * rows, blocks * frames_dev)

    cosine_table, sine_table = fourier_tables()
    with_cos = jnp.dot(arrived, cosine_table, preferred_element_type=jnp.float32)
    with_sin = jnp.dot(arrived, sine_table, preferred_element_type=jnp.float32)
    corr_re = with_cos[:rows] + with_sin[rows:]
    corr_im = with_cos[rows:] - with_sin[:rows]
    correlation = jnp.concatenate([corr_re, corr_im], axis=1).astype(jnp.bfloat16)

    owner = pair_owner[0, :, :, 0].reshape(-1)
    groups = lax.axis_size("chan")
    capacity = max(2, 3 * owner.shape[0] // groups)
    hits = (owner[:, None] == jnp.arange(groups, dtype=jnp.int32)[None, :]).astype(jnp.int32)
    rank = jnp.sum((jnp.cumsum(hits, axis=0) - 1) * hits, axis=1)
    slot = owner * capacity + rank
    placing = (jnp.arange(groups * capacity, dtype=jnp.int32)[:, None] == slot[None, :]).astype(
        jnp.bfloat16
    )
    outgoing = jnp.dot(placing, correlation, preferred_element_type=jnp.float32).astype(
        jnp.bfloat16
    )
    outgoing = outgoing.reshape(groups, capacity, 2 * KEEP)
    arrived = lax.all_to_all(outgoing, "chan", split_axis=0, concat_axis=0, tiled=True)
    return arrived.reshape(1, 1, groups, capacity, 2 * KEEP)


def solution(mesh):
    return jax.shard_map(
        on_device,
        mesh=mesh,
        in_specs=(
            P("chan", "tm"),
            P("tm", "chan", None),
            P("tm", "chan", None),
            P("tm", "chan", None, None),
        ),
        out_specs=P("tm", "chan", None, None, None),
        check_vma=False,
    )
```

```python
import math

import jax
import jax.numpy as jnp
from jax import lax
from jax.sharding import PartitionSpec as P

BANDS = 256
HOP = 64
FRAMES = 2048
KEEP = 1024
DMAX = 8


def passed_along(array, axis, by):
    devices = lax.axis_size(axis)
    pairs = [(i, i + by) for i in range(devices) if 0 <= i + by < devices]
    return lax.ppermute(array, axis, pairs)


def bank_matrix(bands):
    index = jnp.arange(bands, dtype=jnp.int32)
    angle = (index[:, None] * index[None, :] % bands).astype(jnp.float32) * (2.0 * math.pi / bands)
    window = 0.5 - 0.5 * jnp.cos((index.astype(jnp.float32) + 0.5) * (2.0 * math.pi / bands))
    scaled = window / math.sqrt(3.0 * bands / 8.0)
    return jnp.concatenate(
        [scaled[:, None] * jnp.cos(angle), -scaled[:, None] * jnp.sin(angle)], axis=1
    ).astype(jnp.bfloat16)


def turn_table(moments, cycles):
    angle = (moments[:, None] * cycles[None, :] % FRAMES).astype(jnp.float32) * (
        2.0 * math.pi / FRAMES
    )
    return jnp.cos(angle), jnp.sin(angle)


def fourier_tables():
    cycles = jnp.arange(KEEP, dtype=jnp.int32)
    coarse_cos, coarse_sin = turn_table(32 * jnp.arange(FRAMES // 32, dtype=jnp.int32), cycles)
    fine_cos, fine_sin = turn_table(jnp.arange(32, dtype=jnp.int32), cycles)
    scale = 1.0 / math.sqrt(FRAMES)
    cosine = (
        coarse_cos[:, None, :] * fine_cos[None, :, :] - coarse_sin[:, None, :] * fine_sin[None, :, :]
    ) * scale
    sine = (
        coarse_sin[:, None, :] * fine_cos[None, :, :] + coarse_cos[:, None, :] * fine_sin[None, :, :]
    ) * scale
    return (
        cosine.reshape(FRAMES, KEEP).astype(jnp.bfloat16),
        sine.reshape(FRAMES, KEEP).astype(jnp.bfloat16),
    )


def on_device(signal, pair_band, pair_offset, pair_owner):
    channels = signal.shape[0]
    stride_count = BANDS // HOP
    frames_dev = signal.shape[1] // HOP
    blocks = lax.axis_size("tm")
    bank_table = bank_matrix(BANDS)
    sample_tail = passed_along(signal[:, : BANDS - HOP], "tm", -1)
    records = jnp.concatenate([signal, sample_tail], axis=1)
    pieces = records.reshape(channels, frames_dev + stride_count - 1, HOP)
    framed = jnp.concatenate(
        [pieces[:, part_index : part_index + frames_dev, :] for part_index in range(stride_count)],
        axis=2,
    )
    spectra = jnp.einsum(
        "cmn,nk->ckm", framed, bank_table, preferred_element_type=jnp.float32
    ).astype(jnp.bfloat16)
    spectra = spectra.reshape(channels, 2, BANDS, frames_dev)

    local_tables = jnp.stack([pair_band[0], pair_offset[0]], axis=0)
    spread = jnp.broadcast_to(local_tables[None], (blocks,) + local_tables.shape)
    tables = lax.all_to_all(spread, "tm", split_axis=0, concat_axis=0, tiled=True)
    bands_all = tables[:, 0].transpose(1, 0, 2)
    offsets_all = tables[:, 1].transpose(1, 0, 2)
    pairs = bands_all.shape[2]
    band_first = bands_all.reshape(channels, blocks * pairs)
    offset = offsets_all.reshape(channels, blocks * pairs)
    positions = jnp.arange(BANDS, dtype=jnp.int32)
    pick_first = (band_first[..., None] == positions).astype(jnp.bfloat16)
    pick_second = ((band_first + offset)[..., None] == positions).astype(jnp.bfloat16)
    first = jnp.einsum("crb,cpbm->crpm", pick_first, spectra, preferred_element_type=jnp.float32)
    second = jnp.einsum("crb,cpbm->crpm", pick_second, spectra, preferred_element_type=jnp.float32)
    real_part = first[:, :, 0] * second[:, :, 0] + first[:, :, 1] * second[:, :, 1]
    imag_part = first[:, :, 1] * second[:, :, 0] - first[:, :, 0] * second[:, :, 1]

    moment = lax.axis_index("tm") * frames_dev + jnp.arange(frames_dev, dtype=jnp.int32)
    step = math.gcd(HOP * FRAMES // BANDS, KEEP // 2, FRAMES)
    levels = FRAMES // step
    level_cos, level_sin = turn_table(jnp.arange(levels, dtype=jnp.int32), jnp.full((1,), step, jnp.int32))
    shift_bins = (offset * (HOP * FRAMES // BANDS) - KEEP // 2) % FRAMES
    level = (shift_bins[..., None] // step) * moment % levels
    cosine = jnp.full(level.shape, level_cos[0, 0])
    sine = jnp.full(level.shape, level_sin[0, 0])
    for index in range(1, levels):
        chosen = level == index
        cosine = jnp.where(chosen, level_cos[index, 0], cosine)
        sine = jnp.where(chosen, level_sin[index, 0], sine)
    demod_re = (real_part * cosine + imag_part * sine).astype(jnp.bfloat16)
    demod_im = (imag_part * cosine - real_part * sine).astype(jnp.bfloat16)
    demod = jnp.stack([demod_re, demod_im], axis=0)
    demod = demod.reshape(2, channels, blocks, pairs, frames_dev).transpose(0, 1, 3, 2, 4)
    arrived = lax.all_to_all(demod, "tm", split_axis=3, concat_axis=3, tiled=True)
    rows = channels * pairs
    arrived = arrived.reshape(2 * rows, blocks * frames_dev)

    cosine_table, sine_table = fourier_tables()
    with_cos = jnp.dot(arrived, cosine_table, preferred_element_type=jnp.float32)
    with_sin = jnp.dot(arrived, sine_table, preferred_element_type=jnp.float32)
    corr_re = with_cos[:rows] + with_sin[rows:]
    corr_im = with_cos[rows:] - with_sin[:rows]
    correlation = jnp.concatenate([corr_re, corr_im], axis=1).astype(jnp.bfloat16)

    owner = pair_owner[0, :, :, 0].reshape(-1)
    groups = lax.axis_size("chan")
    capacity = max(2, 3 * owner.shape[0] // groups)
    hits = (owner[:, None] == jnp.arange(groups, dtype=jnp.int32)[None, :]).astype(jnp.int32)
    rank = jnp.sum((jnp.cumsum(hits, axis=0) - 1) * hits, axis=1)
    slot = owner * capacity + rank
    placing = (jnp.arange(groups * capacity, dtype=jnp.int32)[:, None] == slot[None, :]).astype(
        jnp.bfloat16
    )
    outgoing = jnp.dot(placing, correlation, preferred_element_type=jnp.float32).astype(
        jnp.bfloat16
    )
    outgoing = outgoing.reshape(groups, capacity, 2 * KEEP)
    arrived = lax.all_to_all(outgoing, "chan", split_axis=0, concat_axis=0, tiled=True)
    return arrived.reshape(1, 1, groups, capacity, 2 * KEEP)


def solution(mesh):
    return jax.shard_map(
        on_device,
        mesh=mesh,
        in_specs=(
            P("chan", "tm"),
            P("tm", "chan", None),
            P("tm", "chan", None),
            P("tm", "chan", None, None),
        ),
        out_specs=P("tm", "chan", None, None, None),
        check_vma=False,
    )
```

```python
import math

import jax
import jax.numpy as jnp
from jax import lax
from jax.sharding import PartitionSpec as P

BANDS = 256
HOP = 64
FRAMES = 2048
KEEP = 1024
DMAX = 8


def passed_along(array, axis, by):
    devices = lax.axis_size(axis)
    pairs = [(i, i + by) for i in range(devices) if 0 <= i + by < devices]
    return lax.ppermute(array, axis, pairs)


def bank_matrix(bands):
    index = jnp.arange(bands, dtype=jnp.int32)
    angle = (index[:, None] * index[None, :] % bands).astype(jnp.float32) * (2.0 * math.pi / bands)
    window = 0.5 - 0.5 * jnp.cos((index.astype(jnp.float32) + 0.5) * (2.0 * math.pi / bands))
    scaled = window / math.sqrt(3.0 * bands / 8.0)
    return jnp.concatenate(
        [scaled[:, None] * jnp.cos(angle), -scaled[:, None] * jnp.sin(angle)], axis=1
    ).astype(jnp.bfloat16)


def turn_table(moments, cycles):
    angle = (moments[:, None] * cycles[None, :] % FRAMES).astype(jnp.float32) * (
        2.0 * math.pi / FRAMES
    )
    return jnp.cos(angle), jnp.sin(angle)


def fourier_tables():
    cycles = jnp.arange(KEEP, dtype=jnp.int32)
    coarse_cos, coarse_sin = turn_table(32 * jnp.arange(FRAMES // 32, dtype=jnp.int32), cycles)
    fine_cos, fine_sin = turn_table(jnp.arange(32, dtype=jnp.int32), cycles)
    scale = 1.0 / math.sqrt(FRAMES)
    cosine = (
        coarse_cos[:, None, :] * fine_cos[None, :, :] - coarse_sin[:, None, :] * fine_sin[None, :, :]
    ) * scale
    sine = (
        coarse_sin[:, None, :] * fine_cos[None, :, :] + coarse_cos[:, None, :] * fine_sin[None, :, :]
    ) * scale
    return (
        cosine.reshape(FRAMES, KEEP).astype(jnp.bfloat16),
        sine.reshape(FRAMES, KEEP).astype(jnp.bfloat16),
    )


def on_device(signal, pair_band, pair_offset, pair_owner):
    channels = signal.shape[0]
    stride_count = BANDS // HOP
    frames_dev = signal.shape[1] // HOP
    blocks = lax.axis_size("tm")
    bank_table = bank_matrix(BANDS)
    sample_tail = passed_along(signal[:, : BANDS - HOP], "tm", -1)
    records = jnp.concatenate([signal, sample_tail], axis=1)
    pieces = records.reshape(channels, frames_dev + stride_count - 1, HOP)
    framed = jnp.concatenate(
        [pieces[:, part_index : part_index + frames_dev, :] for part_index in range(stride_count)],
        axis=2,
    )
    spectra = jnp.einsum(
        "cmn,nk->ckm", framed, bank_table, preferred_element_type=jnp.float32
    ).astype(jnp.bfloat16)
    spectra = spectra.reshape(channels, 2, BANDS, frames_dev)

    local_tables = jnp.stack([pair_band[0], pair_offset[0]], axis=0)
    spread = jnp.broadcast_to(local_tables[None], (blocks,) + local_tables.shape)
    tables = lax.all_to_all(spread, "tm", split_axis=0, concat_axis=0, tiled=True)
    bands_all = tables[:, 0].transpose(1, 0, 2)
    offsets_all = tables[:, 1].transpose(1, 0, 2)
    pairs = bands_all.shape[2]
    band_first = bands_all.reshape(channels, blocks * pairs)
    offset = offsets_all.reshape(channels, blocks * pairs)
    positions = jnp.arange(BANDS, dtype=jnp.int32)
    pick_first = (band_first[..., None] == positions).astype(jnp.bfloat16)
    pick_second = ((band_first + offset)[..., None] == positions).astype(jnp.bfloat16)
    picked = jnp.einsum(
        "crb,cpbm->crpm",
        jnp.concatenate([pick_first, pick_second], axis=1),
        spectra,
        preferred_element_type=jnp.bfloat16,
    ).astype(jnp.float32)
    first = picked[:, : blocks * pairs]
    second = picked[:, blocks * pairs :]
    real_part = first[:, :, 0] * second[:, :, 0] + first[:, :, 1] * second[:, :, 1]
    imag_part = first[:, :, 1] * second[:, :, 0] - first[:, :, 0] * second[:, :, 1]

    moment = lax.axis_index("tm") * frames_dev + jnp.arange(frames_dev, dtype=jnp.int32)
    step = math.gcd(HOP * FRAMES // BANDS, KEEP // 2, FRAMES)
    levels = FRAMES // step
    level_cos, level_sin = turn_table(jnp.arange(levels, dtype=jnp.int32), jnp.full((1,), step, jnp.int32))
    shift_bins = (offset * (HOP * FRAMES // BANDS) - KEEP // 2) % FRAMES
    level = (shift_bins[..., None] // step) * moment % levels
    cosine = jnp.full(level.shape, level_cos[0, 0])
    sine = jnp.full(level.shape, level_sin[0, 0])
    for index in range(1, levels):
        chosen = level == index
        cosine = jnp.where(chosen, level_cos[index, 0], cosine)
        sine = jnp.where(chosen, level_sin[index, 0], sine)
    demod_re = (real_part * cosine + imag_part * sine).astype(jnp.bfloat16)
    demod_im = (imag_part * cosine - real_part * sine).astype(jnp.bfloat16)
    demod = jnp.stack([demod_re, demod_im], axis=0)
    demod = demod.reshape(2, channels, blocks, pairs, frames_dev).transpose(0, 1, 3, 2, 4)
    arrived = lax.all_to_all(demod, "tm", split_axis=3, concat_axis=3, tiled=True)
    rows = channels * pairs
    arrived = arrived.reshape(2 * rows, blocks * frames_dev)

    cosine_table, sine_table = fourier_tables()
    with_cos = jnp.dot(arrived, cosine_table, preferred_element_type=jnp.float32)
    with_sin = jnp.dot(arrived, sine_table, preferred_element_type=jnp.float32)
    corr_re = with_cos[:rows] + with_sin[rows:]
    corr_im = with_cos[rows:] - with_sin[:rows]
    correlation = jnp.concatenate([corr_re, corr_im], axis=1).astype(jnp.bfloat16)

    owner = pair_owner[0, :, :, 0].reshape(-1)
    groups = lax.axis_size("chan")
    capacity = max(2, 3 * owner.shape[0] // groups)
    hits = (owner[:, None] == jnp.arange(groups, dtype=jnp.int32)[None, :]).astype(jnp.int32)
    rank = jnp.sum((jnp.cumsum(hits, axis=0) - 1) * hits, axis=1)
    slot = owner * capacity + rank
    placing = (jnp.arange(groups * capacity, dtype=jnp.int32)[:, None] == slot[None, :]).astype(
        jnp.bfloat16
    )
    outgoing = jnp.dot(placing, correlation, preferred_element_type=jnp.float32).astype(
        jnp.bfloat16
    )
    outgoing = outgoing.reshape(groups, capacity, 2 * KEEP)
    arrived = lax.all_to_all(outgoing, "chan", split_axis=0, concat_axis=0, tiled=True)
    return arrived.reshape(1, 1, groups, capacity, 2 * KEEP)


def solution(mesh):
    return jax.shard_map(
        on_device,
        mesh=mesh,
        in_specs=(
            P("chan", "tm"),
            P("tm", "chan", None),
            P("tm", "chan", None),
            P("tm", "chan", None, None),
        ),
        out_specs=P("tm", "chan", None, None, None),
        check_vma=False,
    )
```

```python
import math

import jax
import jax.numpy as jnp
from jax import lax
from jax.sharding import PartitionSpec as P
from jax.experimental import pallas as pl

BANDS = 256
HOP = 64
FRAMES = 2048
KEEP = 1024
DMAX = 8


def passed_along(array, axis, by):
    devices = lax.axis_size(axis)
    pairs = [(i, i + by) for i in range(devices) if 0 <= i + by < devices]
    return lax.ppermute(array, axis, pairs)


def bank_matrix(bands):
    index = jnp.arange(bands, dtype=jnp.int32)
    angle = (index[:, None] * index[None, :] % bands).astype(jnp.float32) * (2.0 * math.pi / bands)
    window = 0.5 - 0.5 * jnp.cos((index.astype(jnp.float32) + 0.5) * (2.0 * math.pi / bands))
    scaled = window / math.sqrt(3.0 * bands / 8.0)
    return jnp.concatenate(
        [scaled[:, None] * jnp.cos(angle), -scaled[:, None] * jnp.sin(angle)], axis=1
    ).astype(jnp.bfloat16)


def turn_table(moments, cycles):
    angle = (moments[:, None] * cycles[None, :] % FRAMES).astype(jnp.float32) * (
        2.0 * math.pi / FRAMES
    )
    return jnp.cos(angle), jnp.sin(angle)


def fourier_tables():
    cycles = jnp.arange(KEEP, dtype=jnp.int32)
    coarse_cos, coarse_sin = turn_table(32 * jnp.arange(FRAMES // 32, dtype=jnp.int32), cycles)
    fine_cos, fine_sin = turn_table(jnp.arange(32, dtype=jnp.int32), cycles)
    scale = 1.0 / math.sqrt(FRAMES)
    cosine = (
        coarse_cos[:, None, :] * fine_cos[None, :, :] - coarse_sin[:, None, :] * fine_sin[None, :, :]
    ) * scale
    sine = (
        coarse_sin[:, None, :] * fine_cos[None, :, :] + coarse_cos[:, None, :] * fine_sin[None, :, :]
    ) * scale
    return (
        cosine.reshape(FRAMES, KEEP).astype(jnp.bfloat16),
        sine.reshape(FRAMES, KEEP).astype(jnp.bfloat16),
    )


def demod_kernel(spec_ref, first_ref, second_ref, turn_ref, cos_ref, sin_ref, out_ref):
    per_block = spec_ref.shape[0]
    bands = spec_ref.shape[2]
    rows = first_ref.shape[1]
    positions = lax.broadcasted_iota(jnp.int32, (rows, bands), 1)
    for index in range(per_block):
        spectra = jnp.concatenate([spec_ref[index, 0], spec_ref[index, 1]], axis=1)
        pick = jnp.concatenate(
            [
                (first_ref[index] == positions).astype(jnp.bfloat16),
                (second_ref[index] == positions).astype(jnp.bfloat16),
            ],
            axis=0,
        )
        picked = jnp.dot(pick, spectra, preferred_element_type=jnp.float32)
        frames = spectra.shape[1] // 2
        a_re = picked[:rows, :frames]
        a_im = picked[:rows, frames:]
        b_re = picked[rows:, :frames]
        b_im = picked[rows:, frames:]
        real_part = a_re * b_re + a_im * b_im
        imag_part = a_im * b_re - a_re * b_im
        turn = turn_ref[index]
        cosine = jnp.broadcast_to(cos_ref[0:1, :], (rows, frames))
        sine = jnp.broadcast_to(sin_ref[0:1, :], (rows, frames))
        for level in range(1, cos_ref.shape[0]):
            chosen = turn == level
            cosine = jnp.where(chosen, cos_ref[level : level + 1, :], cosine)
            sine = jnp.where(chosen, sin_ref[level : level + 1, :], sine)
        out_ref[0, index] = (real_part * cosine + imag_part * sine).astype(out_ref.dtype)
        out_ref[1, index] = (imag_part * cosine - real_part * sine).astype(out_ref.dtype)


def demodulated(spectra, first, second, turn, cos_table, sin_table, per_block=4, interpret=False):
    channels, parts, bands, frames = spectra.shape
    rows = first.shape[1]
    levels = cos_table.shape[0]
    return pl.pallas_call(
        demod_kernel,
        out_shape=jax.ShapeDtypeStruct((2, channels, rows, frames), jnp.bfloat16),
        grid=(channels // per_block,),
        in_specs=[
            pl.BlockSpec((per_block, parts, bands, frames), lambda i: (i, 0, 0, 0)),
            pl.BlockSpec((per_block, rows, 1), lambda i: (i, 0, 0)),
            pl.BlockSpec((per_block, rows, 1), lambda i: (i, 0, 0)),
            pl.BlockSpec((per_block, rows, 1), lambda i: (i, 0, 0)),
            pl.BlockSpec((levels, frames), lambda i: (0, 0)),
            pl.BlockSpec((levels, frames), lambda i: (0, 0)),
        ],
        out_specs=pl.BlockSpec((2, per_block, rows, frames), lambda i: (0, i, 0, 0)),
        interpret=interpret,
    )(spectra, first[..., None], second[..., None], turn[..., None], cos_table, sin_table)


def on_device(signal, pair_band, pair_offset, pair_owner):
    channels = signal.shape[0]
    stride_count = BANDS // HOP
    frames_dev = signal.shape[1] // HOP
    blocks = lax.axis_size("tm")
    bank_table = bank_matrix(BANDS)
    sample_tail = passed_along(signal[:, : BANDS - HOP], "tm", -1)
    records = jnp.concatenate([signal, sample_tail], axis=1)
    pieces = records.reshape(channels, frames_dev + stride_count - 1, HOP)
    framed = jnp.concatenate(
        [pieces[:, part_index : part_index + frames_dev, :] for part_index in range(stride_count)],
        axis=2,
    )
    spectra = jnp.einsum(
        "cmn,nk->ckm", framed, bank_table, preferred_element_type=jnp.float32
    ).astype(jnp.bfloat16)
    spectra = spectra.reshape(channels, 2, BANDS, frames_dev)

    local_tables = jnp.stack([pair_band[0], pair_offset[0]], axis=0)
    spread = jnp.broadcast_to(local_tables[None], (blocks,) + local_tables.shape)
    tables = lax.all_to_all(spread, "tm", split_axis=0, concat_axis=0, tiled=True)
    bands_all = tables[:, 0].transpose(1, 0, 2)
    offsets_all = tables[:, 1].transpose(1, 0, 2)
    pairs = bands_all.shape[2]
    band_first = bands_all.transpose(0, 2, 1).reshape(channels, pairs * blocks)
    offset = offsets_all.transpose(0, 2, 1).reshape(channels, pairs * blocks)
    moment = lax.axis_index("tm") * frames_dev + jnp.arange(frames_dev, dtype=jnp.int32)
    step = math.gcd(HOP * FRAMES // BANDS, KEEP // 2, FRAMES)
    levels = FRAMES // step
    cos_table, sin_table = turn_table(jnp.arange(levels, dtype=jnp.int32) * step, moment)
    shift_bins = (offset * (HOP * FRAMES // BANDS) - KEEP // 2) % FRAMES
    demod = demodulated(
        spectra, band_first, band_first + offset, shift_bins // step, cos_table, sin_table
    )
    demod = demod.reshape(2, channels, pairs, blocks, frames_dev)
    arrived = lax.all_to_all(demod, "tm", split_axis=3, concat_axis=3, tiled=True)
    rows = channels * pairs
    arrived = arrived.reshape(2 * rows, blocks * frames_dev)

    cosine_table, sine_table = fourier_tables()
    with_cos = jnp.dot(arrived, cosine_table, preferred_element_type=jnp.float32)
    with_sin = jnp.dot(arrived, sine_table, preferred_element_type=jnp.float32)
    corr_re = with_cos[:rows] + with_sin[rows:]
    corr_im = with_cos[rows:] - with_sin[:rows]
    correlation = jnp.concatenate([corr_re, corr_im], axis=1).astype(jnp.bfloat16)

    owner = pair_owner[0, :, :, 0].reshape(-1)
    groups = lax.axis_size("chan")
    capacity = max(2, 3 * owner.shape[0] // groups)
    hits = (owner[:, None] == jnp.arange(groups, dtype=jnp.int32)[None, :]).astype(jnp.int32)
    rank = jnp.sum((jnp.cumsum(hits, axis=0) - 1) * hits, axis=1)
    slot = owner * capacity + rank
    placing = (jnp.arange(groups * capacity, dtype=jnp.int32)[:, None] == slot[None, :]).astype(
        jnp.bfloat16
    )
    outgoing = jnp.dot(placing, correlation, preferred_element_type=jnp.float32).astype(
        jnp.bfloat16
    )
    outgoing = outgoing.reshape(groups, capacity, 2 * KEEP)
    arrived = lax.all_to_all(outgoing, "chan", split_axis=0, concat_axis=0, tiled=True)
    return arrived.reshape(1, 1, groups, capacity, 2 * KEEP)


def solution(mesh):
    return jax.shard_map(
        on_device,
        mesh=mesh,
        in_specs=(
            P("chan", "tm"),
            P("tm", "chan", None),
            P("tm", "chan", None),
            P("tm", "chan", None, None),
        ),
        out_specs=P("tm", "chan", None, None, None),
        check_vma=False,
    )
```

```python
import math

import jax
import jax.numpy as jnp
from jax import lax
from jax.sharding import PartitionSpec as P
from jax.experimental import pallas as pl

BANDS = 256
HOP = 64
FRAMES = 2048
KEEP = 1024
DMAX = 8


def passed_along(array, axis, by):
    devices = lax.axis_size(axis)
    pairs = [(i, i + by) for i in range(devices) if 0 <= i + by < devices]
    return lax.ppermute(array, axis, pairs)


def bank_matrix(bands):
    index = jnp.arange(bands, dtype=jnp.int32)
    angle = (index[:, None] * index[None, :] % bands).astype(jnp.float32) * (2.0 * math.pi / bands)
    window = 0.5 - 0.5 * jnp.cos((index.astype(jnp.float32) + 0.5) * (2.0 * math.pi / bands))
    scaled = window / math.sqrt(3.0 * bands / 8.0)
    return jnp.concatenate(
        [scaled[:, None] * jnp.cos(angle), -scaled[:, None] * jnp.sin(angle)], axis=1
    ).astype(jnp.bfloat16)


def turn_table(moments, cycles):
    angle = (moments[:, None] * cycles[None, :] % FRAMES).astype(jnp.float32) * (
        2.0 * math.pi / FRAMES
    )
    return jnp.cos(angle), jnp.sin(angle)


def fourier_tables():
    cycles = jnp.arange(KEEP, dtype=jnp.int32)
    coarse_cos, coarse_sin = turn_table(32 * jnp.arange(FRAMES // 32, dtype=jnp.int32), cycles)
    fine_cos, fine_sin = turn_table(jnp.arange(32, dtype=jnp.int32), cycles)
    scale = 1.0 / math.sqrt(FRAMES)
    cosine = (
        coarse_cos[:, None, :] * fine_cos[None, :, :] - coarse_sin[:, None, :] * fine_sin[None, :, :]
    ) * scale
    sine = (
        coarse_sin[:, None, :] * fine_cos[None, :, :] + coarse_cos[:, None, :] * fine_sin[None, :, :]
    ) * scale
    return (
        cosine.reshape(FRAMES, KEEP).astype(jnp.bfloat16),
        sine.reshape(FRAMES, KEEP).astype(jnp.bfloat16),
    )


def demod_kernel(spec_ref, first_ref, second_ref, turn_ref, cos_ref, sin_ref, out_ref):
    per_block = spec_ref.shape[0]
    bands = spec_ref.shape[2]
    frames = spec_ref.shape[3]
    rows = first_ref.shape[1]
    blocks = out_ref.shape[0]
    pairs = out_ref.shape[3]
    positions = lax.broadcasted_iota(jnp.int32, (rows, bands), 1)
    first_all = first_ref[...].T
    second_all = second_ref[...].T
    turn_all = turn_ref[...].T
    for index in range(per_block):
        spectra = jnp.concatenate([spec_ref[index, 0], spec_ref[index, 1]], axis=1)
        pick = jnp.concatenate(
            [
                (first_all[:, index : index + 1] == positions).astype(jnp.bfloat16),
                (second_all[:, index : index + 1] == positions).astype(jnp.bfloat16),
            ],
            axis=0,
        )
        picked = jnp.dot(pick, spectra, preferred_element_type=jnp.float32)
        a_re = picked[:rows, :frames]
        a_im = picked[:rows, frames:]
        b_re = picked[rows:, :frames]
        b_im = picked[rows:, frames:]
        real_part = a_re * b_re + a_im * b_im
        imag_part = a_im * b_re - a_re * b_im
        turn = turn_all[:, index : index + 1]
        cosine = jnp.broadcast_to(cos_ref[0:1, :], (rows, frames))
        sine = jnp.broadcast_to(sin_ref[0:1, :], (rows, frames))
        for level in range(1, cos_ref.shape[0]):
            chosen = turn == level
            cosine = jnp.where(chosen, cos_ref[level : level + 1, :], cosine)
            sine = jnp.where(chosen, sin_ref[level : level + 1, :], sine)
        demod_re = (real_part * cosine + imag_part * sine).astype(out_ref.dtype)
        demod_im = (imag_part * cosine - real_part * sine).astype(out_ref.dtype)
        for block in range(blocks):
            out_ref[block, 0, index] = demod_re[block * pairs : (block + 1) * pairs]
            out_ref[block, 1, index] = demod_im[block * pairs : (block + 1) * pairs]


def demodulated(spectra, first, second, turn, cos_table, sin_table, blocks, per_block=8, interpret=False):
    channels, parts, bands, frames = spectra.shape
    rows = first.shape[1]
    pairs = rows // blocks
    levels = cos_table.shape[0]
    return pl.pallas_call(
        demod_kernel,
        out_shape=jax.ShapeDtypeStruct((blocks, 2, channels, pairs, frames), jnp.bfloat16),
        grid=(channels // per_block,),
        in_specs=[
            pl.BlockSpec((per_block, parts, bands, frames), lambda i: (i, 0, 0, 0)),
            pl.BlockSpec((per_block, rows), lambda i: (i, 0)),
            pl.BlockSpec((per_block, rows), lambda i: (i, 0)),
            pl.BlockSpec((per_block, rows), lambda i: (i, 0)),
            pl.BlockSpec((levels, frames), lambda i: (0, 0)),
            pl.BlockSpec((levels, frames), lambda i: (0, 0)),
        ],
        out_specs=pl.BlockSpec((blocks, 2, per_block, pairs, frames), lambda i: (0, 0, i, 0, 0)),
        interpret=interpret,
    )(spectra, first, second, turn, cos_table, sin_table)


def on_device(signal, pair_band, pair_offset, pair_owner):
    channels = signal.shape[0]
    stride_count = BANDS // HOP
    frames_dev = signal.shape[1] // HOP
    blocks = lax.axis_size("tm")
    bank_table = bank_matrix(BANDS)
    sample_tail = passed_along(signal[:, : BANDS - HOP], "tm", -1)
    records = jnp.concatenate([signal, sample_tail], axis=1)
    pieces = records.reshape(channels, frames_dev + stride_count - 1, HOP)
    framed = jnp.concatenate(
        [pieces[:, part_index : part_index + frames_dev, :] for part_index in range(stride_count)],
        axis=2,
    )
    spectra = jnp.einsum(
        "cmn,nk->ckm", framed, bank_table, preferred_element_type=jnp.float32
    ).astype(jnp.bfloat16)
    spectra = spectra.reshape(channels, 2, BANDS, frames_dev)

    local_tables = jnp.stack([pair_band[0], pair_offset[0]], axis=0)
    spread = jnp.broadcast_to(local_tables[None], (blocks,) + local_tables.shape)
    tables = lax.all_to_all(spread, "tm", split_axis=0, concat_axis=0, tiled=True)
    bands_all = tables[:, 0].transpose(1, 0, 2)
    offsets_all = tables[:, 1].transpose(1, 0, 2)
    pairs = bands_all.shape[2]
    band_first = bands_all.reshape(channels, blocks * pairs)
    offset = offsets_all.reshape(channels, blocks * pairs)
    moment = lax.axis_index("tm") * frames_dev + jnp.arange(frames_dev, dtype=jnp.int32)
    step = math.gcd(HOP * FRAMES // BANDS, KEEP // 2, FRAMES)
    levels = FRAMES // step
    cos_table, sin_table = turn_table(jnp.arange(levels, dtype=jnp.int32) * step, moment)
    shift_bins = (offset * (HOP * FRAMES // BANDS) - KEEP // 2) % FRAMES
    demod = demodulated(
        spectra, band_first, band_first + offset, shift_bins // step, cos_table, sin_table, blocks
    )
    arrived = lax.all_to_all(demod, "tm", split_axis=0, concat_axis=0, tiled=True)
    arrived = arrived.transpose(1, 2, 3, 0, 4)
    rows = channels * pairs
    arrived = arrived.reshape(2 * rows, blocks * frames_dev)

    cosine_table, sine_table = fourier_tables()
    with_cos = jnp.dot(arrived, cosine_table, preferred_element_type=jnp.float32)
    with_sin = jnp.dot(arrived, sine_table, preferred_element_type=jnp.float32)
    corr_re = with_cos[:rows] + with_sin[rows:]
    corr_im = with_cos[rows:] - with_sin[:rows]
    correlation = jnp.concatenate([corr_re, corr_im], axis=1).astype(jnp.bfloat16)

    owner = pair_owner[0, :, :, 0].reshape(-1)
    groups = lax.axis_size("chan")
    capacity = max(2, 3 * owner.shape[0] // groups)
    hits = (owner[:, None] == jnp.arange(groups, dtype=jnp.int32)[None, :]).astype(jnp.int32)
    rank = jnp.sum((jnp.cumsum(hits, axis=0) - 1) * hits, axis=1)
    slot = owner * capacity + rank
    placing = (jnp.arange(groups * capacity, dtype=jnp.int32)[:, None] == slot[None, :]).astype(
        jnp.bfloat16
    )
    outgoing = jnp.dot(placing, correlation, preferred_element_type=jnp.float32).astype(
        jnp.bfloat16
    )
    outgoing = outgoing.reshape(groups, capacity, 2 * KEEP)
    arrived = lax.all_to_all(outgoing, "chan", split_axis=0, concat_axis=0, tiled=True)
    return arrived.reshape(1, 1, groups, capacity, 2 * KEEP)


def solution(mesh):
    return jax.shard_map(
        on_device,
        mesh=mesh,
        in_specs=(
            P("chan", "tm"),
            P("tm", "chan", None),
            P("tm", "chan", None),
            P("tm", "chan", None, None),
        ),
        out_specs=P("tm", "chan", None, None, None),
        check_vma=False,
    )
```

```python
import math

import jax
import jax.numpy as jnp
from jax import lax
from jax.sharding import PartitionSpec as P
from jax.experimental import pallas as pl

BANDS = 256
HOP = 64
FRAMES = 2048
KEEP = 1024
DMAX = 8


def passed_along(array, axis, by):
    devices = lax.axis_size(axis)
    pairs = [(i, i + by) for i in range(devices) if 0 <= i + by < devices]
    return lax.ppermute(array, axis, pairs)


def bank_matrix(bands):
    index = jnp.arange(bands, dtype=jnp.int32)
    angle = (index[:, None] * index[None, :] % bands).astype(jnp.float32) * (2.0 * math.pi / bands)
    window = 0.5 - 0.5 * jnp.cos((index.astype(jnp.float32) + 0.5) * (2.0 * math.pi / bands))
    scaled = window / math.sqrt(3.0 * bands / 8.0)
    return jnp.concatenate(
        [scaled[:, None] * jnp.cos(angle), -scaled[:, None] * jnp.sin(angle)], axis=1
    ).astype(jnp.bfloat16)


def turn_table(moments, cycles):
    angle = (moments[:, None] * cycles[None, :] % FRAMES).astype(jnp.float32) * (
        2.0 * math.pi / FRAMES
    )
    return jnp.cos(angle), jnp.sin(angle)


def fourier_tables():
    cycles = jnp.arange(KEEP, dtype=jnp.int32)
    coarse_cos, coarse_sin = turn_table(32 * jnp.arange(FRAMES // 32, dtype=jnp.int32), cycles)
    fine_cos, fine_sin = turn_table(jnp.arange(32, dtype=jnp.int32), cycles)
    scale = 1.0 / math.sqrt(FRAMES)
    cosine = (
        coarse_cos[:, None, :] * fine_cos[None, :, :] - coarse_sin[:, None, :] * fine_sin[None, :, :]
    ) * scale
    sine = (
        coarse_sin[:, None, :] * fine_cos[None, :, :] + coarse_cos[:, None, :] * fine_sin[None, :, :]
    ) * scale
    return (
        cosine.reshape(FRAMES, KEEP).astype(jnp.bfloat16),
        sine.reshape(FRAMES, KEEP).astype(jnp.bfloat16),
    )


def demod_kernel(framed_ref, bank_ref, first_ref, second_ref, turn_ref, cos_ref, sin_ref, out_ref):
    per_block = framed_ref.shape[0]
    frames = framed_ref.shape[1]
    bands = bank_ref.shape[0] // 2
    rows = first_ref.shape[1]
    blocks = out_ref.shape[0]
    pairs = out_ref.shape[3]
    positions = lax.broadcasted_iota(jnp.int32, (rows, bands), 1)
    first_all = first_ref[...].T
    second_all = second_ref[...].T
    turn_all = turn_ref[...].T
    for index in range(per_block):
        spectra = lax.dot_general(
            bank_ref[...], framed_ref[index], (((1,), (1,)), ((), ())),
            preferred_element_type=jnp.float32,
        ).astype(jnp.bfloat16)
        spectra = jnp.concatenate([spectra[:bands], spectra[bands:]], axis=1)
        pick = jnp.concatenate(
            [
                (first_all[:, index : index + 1] == positions).astype(jnp.bfloat16),
                (second_all[:, index : index + 1] == positions).astype(jnp.bfloat16),
            ],
            axis=0,
        )
        picked = jnp.dot(pick, spectra, preferred_element_type=jnp.float32)
        a_re = picked[:rows, :frames]
        a_im = picked[:rows, frames:]
        b_re = picked[rows:, :frames]
        b_im = picked[rows:, frames:]
        real_part = a_re * b_re + a_im * b_im
        imag_part = a_im * b_re - a_re * b_im
        turn = turn_all[:, index : index + 1]
        cosine = jnp.broadcast_to(cos_ref[0:1, :], (rows, frames))
        sine = jnp.broadcast_to(sin_ref[0:1, :], (rows, frames))
        for level in range(1, cos_ref.shape[0]):
            chosen = turn == level
            cosine = jnp.where(chosen, cos_ref[level : level + 1, :], cosine)
            sine = jnp.where(chosen, sin_ref[level : level + 1, :], sine)
        demod_re = (real_part * cosine + imag_part * sine).astype(out_ref.dtype)
        demod_im = (imag_part * cosine - real_part * sine).astype(out_ref.dtype)
        for block in range(blocks):
            out_ref[block, 0, index] = demod_re[block * pairs : (block + 1) * pairs]
            out_ref[block, 1, index] = demod_im[block * pairs : (block + 1) * pairs]


def demodulated(framed, bank, first, second, turn, cos_table, sin_table, blocks, per_block=8, interpret=False):
    channels, frames, window = framed.shape
    rows = first.shape[1]
    pairs = rows // blocks
    levels = cos_table.shape[0]
    return pl.pallas_call(
        demod_kernel,
        out_shape=jax.ShapeDtypeStruct((blocks, 2, channels, pairs, frames), jnp.bfloat16),
        grid=(channels // per_block,),
        in_specs=[
            pl.BlockSpec((per_block, frames, window), lambda i: (i, 0, 0)),
            pl.BlockSpec(bank.shape, lambda i: (0, 0)),
            pl.BlockSpec((per_block, rows), lambda i: (i, 0)),
            pl.BlockSpec((per_block, rows), lambda i: (i, 0)),
            pl.BlockSpec((per_block, rows), lambda i: (i, 0)),
            pl.BlockSpec((levels, frames), lambda i: (0, 0)),
            pl.BlockSpec((levels, frames), lambda i: (0, 0)),
        ],
        out_specs=pl.BlockSpec((blocks, 2, per_block, pairs, frames), lambda i: (0, 0, i, 0, 0)),
        interpret=interpret,
    )(framed, bank, first, second, turn, cos_table, sin_table)


def on_device(signal, pair_band, pair_offset, pair_owner):
    channels = signal.shape[0]
    stride_count = BANDS // HOP
    frames_dev = signal.shape[1] // HOP
    blocks = lax.axis_size("tm")
    bank_table = bank_matrix(BANDS)
    sample_tail = passed_along(signal[:, : BANDS - HOP], "tm", -1)
    records = jnp.concatenate([signal, sample_tail], axis=1)
    pieces = records.reshape(channels, frames_dev + stride_count - 1, HOP)
    framed = jnp.concatenate(
        [pieces[:, part_index : part_index + frames_dev, :] for part_index in range(stride_count)],
        axis=2,
    )

    local_tables = jnp.stack([pair_band[0], pair_offset[0]], axis=0)
    spread = jnp.broadcast_to(local_tables[None], (blocks,) + local_tables.shape)
    tables = lax.all_to_all(spread, "tm", split_axis=0, concat_axis=0, tiled=True)
    bands_all = tables[:, 0].transpose(1, 0, 2)
    offsets_all = tables[:, 1].transpose(1, 0, 2)
    pairs = bands_all.shape[2]
    band_first = bands_all.reshape(channels, blocks * pairs)
    offset = offsets_all.reshape(channels, blocks * pairs)
    moment = lax.axis_index("tm") * frames_dev + jnp.arange(frames_dev, dtype=jnp.int32)
    step = math.gcd(HOP * FRAMES // BANDS, KEEP // 2, FRAMES)
    levels = FRAMES // step
    cos_table, sin_table = turn_table(jnp.arange(levels, dtype=jnp.int32) * step, moment)
    shift_bins = (offset * (HOP * FRAMES // BANDS) - KEEP // 2) % FRAMES
    demod = demodulated(
        framed, bank_table.T, band_first, band_first + offset, shift_bins // step,
        cos_table, sin_table, blocks,
    )
    arrived = lax.all_to_all(demod, "tm", split_axis=0, concat_axis=0, tiled=True)
    arrived = arrived.transpose(1, 2, 3, 0, 4)
    rows = channels * pairs
    arrived = arrived.reshape(2 * rows, blocks * frames_dev)

    cosine_table, sine_table = fourier_tables()
    with_cos = jnp.dot(arrived, cosine_table, preferred_element_type=jnp.float32)
    with_sin = jnp.dot(arrived, sine_table, preferred_element_type=jnp.float32)
    corr_re = with_cos[:rows] + with_sin[rows:]
    corr_im = with_cos[rows:] - with_sin[:rows]
    correlation = jnp.concatenate([corr_re, corr_im], axis=1).astype(jnp.bfloat16)

    owner = pair_owner[0, :, :, 0].reshape(-1)
    groups = lax.axis_size("chan")
    capacity = max(2, 3 * owner.shape[0] // groups)
    hits = (owner[:, None] == jnp.arange(groups, dtype=jnp.int32)[None, :]).astype(jnp.int32)
    rank = jnp.sum((jnp.cumsum(hits, axis=0) - 1) * hits, axis=1)
    slot = owner * capacity + rank
    placing = (jnp.arange(groups * capacity, dtype=jnp.int32)[:, None] == slot[None, :]).astype(
        jnp.bfloat16
    )
    outgoing = jnp.dot(placing, correlation, preferred_element_type=jnp.float32).astype(
        jnp.bfloat16
    )
    outgoing = outgoing.reshape(groups, capacity, 2 * KEEP)
    arrived = lax.all_to_all(outgoing, "chan", split_axis=0, concat_axis=0, tiled=True)
    return arrived.reshape(1, 1, groups, capacity, 2 * KEEP)


def solution(mesh):
    return jax.shard_map(
        on_device,
        mesh=mesh,
        in_specs=(
            P("chan", "tm"),
            P("tm", "chan", None),
            P("tm", "chan", None),
            P("tm", "chan", None, None),
        ),
        out_specs=P("tm", "chan", None, None, None),
        check_vma=False,
    )
```

```python
import math

import jax
import jax.numpy as jnp
from jax import lax
from jax.sharding import PartitionSpec as P
from jax.experimental import pallas as pl

BANDS = 256
HOP = 64
FRAMES = 2048
KEEP = 1024
DMAX = 8


def passed_along(array, axis, by):
    devices = lax.axis_size(axis)
    pairs = [(i, i + by) for i in range(devices) if 0 <= i + by < devices]
    return lax.ppermute(array, axis, pairs)


def bank_matrix(bands):
    index = jnp.arange(bands, dtype=jnp.int32)
    angle = (index[:, None] * index[None, :] % bands).astype(jnp.float32) * (2.0 * math.pi / bands)
    window = 0.5 - 0.5 * jnp.cos((index.astype(jnp.float32) + 0.5) * (2.0 * math.pi / bands))
    scaled = window / math.sqrt(3.0 * bands / 8.0)
    return jnp.concatenate(
        [scaled[:, None] * jnp.cos(angle), -scaled[:, None] * jnp.sin(angle)], axis=1
    ).astype(jnp.bfloat16)


def turn_table(moments, cycles):
    angle = (moments[:, None] * cycles[None, :] % FRAMES).astype(jnp.float32) * (
        2.0 * math.pi / FRAMES
    )
    return jnp.cos(angle), jnp.sin(angle)


def fourier_tables():
    cycles = jnp.arange(KEEP, dtype=jnp.int32)
    coarse_cos, coarse_sin = turn_table(32 * jnp.arange(FRAMES // 32, dtype=jnp.int32), cycles)
    fine_cos, fine_sin = turn_table(jnp.arange(32, dtype=jnp.int32), cycles)
    scale = 1.0 / math.sqrt(FRAMES)
    cosine = (
        coarse_cos[:, None, :] * fine_cos[None, :, :] - coarse_sin[:, None, :] * fine_sin[None, :, :]
    ) * scale
    sine = (
        coarse_sin[:, None, :] * fine_cos[None, :, :] + coarse_cos[:, None, :] * fine_sin[None, :, :]
    ) * scale
    return (
        cosine.reshape(FRAMES, KEEP).astype(jnp.bfloat16),
        sine.reshape(FRAMES, KEEP).astype(jnp.bfloat16),
    )


def demod_kernel(spec_ref, first_ref, second_ref, turn_ref, cos_ref, sin_ref, out_ref):
    per_block = spec_ref.shape[0]
    bands = spec_ref.shape[2]
    frames = spec_ref.shape[3]
    rows = first_ref.shape[1]
    blocks = out_ref.shape[0]
    pairs = out_ref.shape[3]
    positions = lax.broadcasted_iota(jnp.int32, (rows, bands), 1)
    first_all = first_ref[...].T
    second_all = second_ref[...].T
    turn_all = turn_ref[...].T
    for index in range(per_block):
        spectra = jnp.concatenate([spec_ref[index, 0], spec_ref[index, 1]], axis=1)
        pick = jnp.concatenate(
            [
                (first_all[:, index : index + 1] == positions).astype(jnp.bfloat16),
                (second_all[:, index : index + 1] == positions).astype(jnp.bfloat16),
            ],
            axis=0,
        )
        picked = jnp.dot(pick, spectra, preferred_element_type=jnp.float32)
        a_re = picked[:rows, :frames]
        a_im = picked[:rows, frames:]
        b_re = picked[rows:, :frames]
        b_im = picked[rows:, frames:]
        real_part = a_re * b_re + a_im * b_im
        imag_part = a_im * b_re - a_re * b_im
        turn = turn_all[:, index : index + 1]
        cosine = jnp.broadcast_to(cos_ref[0:1, :], (rows, frames))
        sine = jnp.broadcast_to(sin_ref[0:1, :], (rows, frames))
        for level in range(1, cos_ref.shape[0]):
            chosen = turn == level
            cosine = jnp.where(chosen, cos_ref[level : level + 1, :], cosine)
            sine = jnp.where(chosen, sin_ref[level : level + 1, :], sine)
        demod_re = (real_part * cosine + imag_part * sine).astype(out_ref.dtype)
        demod_im = (imag_part * cosine - real_part * sine).astype(out_ref.dtype)
        for block in range(blocks):
            out_ref[block, 0, index] = demod_re[block * pairs : (block + 1) * pairs]
            out_ref[block, 1, index] = demod_im[block * pairs : (block + 1) * pairs]


def demodulated(spectra, first, second, turn, cos_table, sin_table, blocks, per_block=8, interpret=False):
    channels, parts, bands, frames = spectra.shape
    rows = first.shape[1]
    pairs = rows // blocks
    levels = cos_table.shape[0]
    return pl.pallas_call(
        demod_kernel,
        out_shape=jax.ShapeDtypeStruct((blocks, 2, channels, pairs, frames), jnp.bfloat16),
        grid=(channels // per_block,),
        in_specs=[
            pl.BlockSpec((per_block, parts, bands, frames), lambda i: (i, 0, 0, 0)),
            pl.BlockSpec((per_block, rows), lambda i: (i, 0)),
            pl.BlockSpec((per_block, rows), lambda i: (i, 0)),
            pl.BlockSpec((per_block, rows), lambda i: (i, 0)),
            pl.BlockSpec((levels, frames), lambda i: (0, 0)),
            pl.BlockSpec((levels, frames), lambda i: (0, 0)),
        ],
        out_specs=pl.BlockSpec((blocks, 2, per_block, pairs, frames), lambda i: (0, 0, i, 0, 0)),
        interpret=interpret,
    )(spectra, first, second, turn, cos_table, sin_table)


def on_device(signal, pair_band, pair_offset, pair_owner):
    channels = signal.shape[0]
    stride_count = BANDS // HOP
    frames_dev = signal.shape[1] // HOP
    blocks = lax.axis_size("tm")
    bank_table = bank_matrix(BANDS)
    sample_tail = passed_along(signal[:, : BANDS - HOP], "tm", -1)
    records = jnp.concatenate([signal, sample_tail], axis=1)
    pieces = records.reshape(channels, frames_dev + stride_count - 1, HOP)
    framed = jnp.concatenate(
        [pieces[:, part_index : part_index + frames_dev, :] for part_index in range(stride_count)],
        axis=2,
    )
    spectra = jnp.einsum(
        "cmn,nk->ckm", framed, bank_table, preferred_element_type=jnp.float32
    ).astype(jnp.bfloat16)
    spectra = spectra.reshape(channels, 2, BANDS, frames_dev)

    local_tables = jnp.stack([pair_band[0], pair_offset[0]], axis=0)
    spectra, local_tables = lax.optimization_barrier((spectra, local_tables))
    spread = jnp.broadcast_to(local_tables[None], (blocks,) + local_tables.shape)
    tables = lax.all_to_all(spread, "tm", split_axis=0, concat_axis=0, tiled=True)
    bands_all = tables[:, 0].transpose(1, 0, 2)
    offsets_all = tables[:, 1].transpose(1, 0, 2)
    pairs = bands_all.shape[2]
    band_first = bands_all.reshape(channels, blocks * pairs)
    offset = offsets_all.reshape(channels, blocks * pairs)
    moment = lax.axis_index("tm") * frames_dev + jnp.arange(frames_dev, dtype=jnp.int32)
    step = math.gcd(HOP * FRAMES // BANDS, KEEP // 2, FRAMES)
    levels = FRAMES // step
    cos_table, sin_table = turn_table(jnp.arange(levels, dtype=jnp.int32) * step, moment)
    shift_bins = (offset * (HOP * FRAMES // BANDS) - KEEP // 2) % FRAMES
    demod = demodulated(
        spectra, band_first, band_first + offset, shift_bins // step, cos_table, sin_table, blocks
    )
    arrived = lax.all_to_all(demod, "tm", split_axis=0, concat_axis=0, tiled=True)
    arrived = arrived.transpose(1, 2, 3, 0, 4)
    rows = channels * pairs
    arrived = arrived.reshape(2 * rows, blocks * frames_dev)

    cosine_table, sine_table = fourier_tables()
    with_cos = jnp.dot(arrived, cosine_table, preferred_element_type=jnp.float32)
    with_sin = jnp.dot(arrived, sine_table, preferred_element_type=jnp.float32)
    corr_re = with_cos[:rows] + with_sin[rows:]
    corr_im = with_cos[rows:] - with_sin[:rows]
    correlation = jnp.concatenate([corr_re, corr_im], axis=1).astype(jnp.bfloat16)

    owner = pair_owner[0, :, :, 0].reshape(-1)
    groups = lax.axis_size("chan")
    capacity = max(2, 3 * owner.shape[0] // groups)
    hits = (owner[:, None] == jnp.arange(groups, dtype=jnp.int32)[None, :]).astype(jnp.int32)
    rank = jnp.sum((jnp.cumsum(hits, axis=0) - 1) * hits, axis=1)
    slot = owner * capacity + rank
    placing = (jnp.arange(groups * capacity, dtype=jnp.int32)[:, None] == slot[None, :]).astype(
        jnp.bfloat16
    )
    outgoing = jnp.dot(placing, correlation, preferred_element_type=jnp.float32).astype(
        jnp.bfloat16
    )
    outgoing = outgoing.reshape(groups, capacity, 2 * KEEP)
    arrived = lax.all_to_all(outgoing, "chan", split_axis=0, concat_axis=0, tiled=True)
    return arrived.reshape(1, 1, groups, capacity, 2 * KEEP)


def solution(mesh):
    return jax.shard_map(
        on_device,
        mesh=mesh,
        in_specs=(
            P("chan", "tm"),
            P("tm", "chan", None),
            P("tm", "chan", None),
            P("tm", "chan", None, None),
        ),
        out_specs=P("tm", "chan", None, None, None),
        check_vma=False,
    )
```

```python
import math

import jax
import jax.numpy as jnp
from jax import lax
from jax.sharding import PartitionSpec as P
from jax.experimental import pallas as pl

BANDS = 256
HOP = 64
FRAMES = 2048
KEEP = 1024
DMAX = 8


def passed_along(array, axis, by):
    devices = lax.axis_size(axis)
    pairs = [(i, i + by) for i in range(devices) if 0 <= i + by < devices]
    return lax.ppermute(array, axis, pairs)


def bank_matrix(bands):
    index = jnp.arange(bands, dtype=jnp.int32)
    angle = (index[:, None] * index[None, :] % bands).astype(jnp.float32) * (2.0 * math.pi / bands)
    window = 0.5 - 0.5 * jnp.cos((index.astype(jnp.float32) + 0.5) * (2.0 * math.pi / bands))
    scaled = window / math.sqrt(3.0 * bands / 8.0)
    return jnp.concatenate(
        [scaled[:, None] * jnp.cos(angle), -scaled[:, None] * jnp.sin(angle)], axis=1
    ).astype(jnp.bfloat16)


def turn_table(moments, cycles):
    angle = (moments[:, None] * cycles[None, :] % FRAMES).astype(jnp.float32) * (
        2.0 * math.pi / FRAMES
    )
    return jnp.cos(angle), jnp.sin(angle)


def fourier_tables():
    cycles = jnp.arange(KEEP, dtype=jnp.int32)
    coarse_cos, coarse_sin = turn_table(32 * jnp.arange(FRAMES // 32, dtype=jnp.int32), cycles)
    fine_cos, fine_sin = turn_table(jnp.arange(32, dtype=jnp.int32), cycles)
    scale = 1.0 / math.sqrt(FRAMES)
    cosine = (
        coarse_cos[:, None, :] * fine_cos[None, :, :] - coarse_sin[:, None, :] * fine_sin[None, :, :]
    ) * scale
    sine = (
        coarse_sin[:, None, :] * fine_cos[None, :, :] + coarse_cos[:, None, :] * fine_sin[None, :, :]
    ) * scale
    return (
        cosine.reshape(FRAMES, KEEP).astype(jnp.bfloat16),
        sine.reshape(FRAMES, KEEP).astype(jnp.bfloat16),
    )


def demod_kernel(spec_ref, first_ref, second_ref, turn_ref, cos_ref, sin_ref, out_ref):
    per_block = spec_ref.shape[0]
    bands = spec_ref.shape[2]
    frames = spec_ref.shape[3]
    rows = first_ref.shape[1]
    blocks = out_ref.shape[0]
    pairs = out_ref.shape[3]
    positions = lax.broadcasted_iota(jnp.int32, (rows, bands), 1)
    first_all = first_ref[...].T
    second_all = second_ref[...].T
    turn_all = turn_ref[...].T
    for index in range(per_block):
        spectra = jnp.concatenate([spec_ref[index, 0], spec_ref[index, 1]], axis=1)
        pick = jnp.concatenate(
            [
                (first_all[:, index : index + 1] == positions).astype(jnp.bfloat16),
                (second_all[:, index : index + 1] == positions).astype(jnp.bfloat16),
            ],
            axis=0,
        )
        picked = jnp.dot(pick, spectra, preferred_element_type=jnp.float32)
        a_re = picked[:rows, :frames]
        a_im = picked[:rows, frames:]
        b_re = picked[rows:, :frames]
        b_im = picked[rows:, frames:]
        real_part = a_re * b_re + a_im * b_im
        imag_part = a_im * b_re - a_re * b_im
        turn = turn_all[:, index : index + 1]
        cosine = jnp.broadcast_to(cos_ref[0:1, :], (rows, frames))
        sine = jnp.broadcast_to(sin_ref[0:1, :], (rows, frames))
        for level in range(1, cos_ref.shape[0]):
            chosen = turn == level
            cosine = jnp.where(chosen, cos_ref[level : level + 1, :], cosine)
            sine = jnp.where(chosen, sin_ref[level : level + 1, :], sine)
        demod_re = (real_part * cosine + imag_part * sine).astype(out_ref.dtype)
        demod_im = (imag_part * cosine - real_part * sine).astype(out_ref.dtype)
        for block in range(blocks):
            out_ref[block, 0, index] = demod_re[block * pairs : (block + 1) * pairs]
            out_ref[block, 1, index] = demod_im[block * pairs : (block + 1) * pairs]


def demodulated(spectra, first, second, turn, cos_table, sin_table, blocks, per_block=8, interpret=False):
    channels, parts, bands, frames = spectra.shape
    rows = first.shape[1]
    pairs = rows // blocks
    levels = cos_table.shape[0]
    return pl.pallas_call(
        demod_kernel,
        out_shape=jax.ShapeDtypeStruct((blocks, 2, channels, pairs, frames), jnp.bfloat16),
        grid=(channels // per_block,),
        in_specs=[
            pl.BlockSpec((per_block, parts, bands, frames), lambda i: (i, 0, 0, 0)),
            pl.BlockSpec((per_block, rows), lambda i: (i, 0)),
            pl.BlockSpec((per_block, rows), lambda i: (i, 0)),
            pl.BlockSpec((per_block, rows), lambda i: (i, 0)),
            pl.BlockSpec((levels, frames), lambda i: (0, 0)),
            pl.BlockSpec((levels, frames), lambda i: (0, 0)),
        ],
        out_specs=pl.BlockSpec((blocks, 2, per_block, pairs, frames), lambda i: (0, 0, i, 0, 0)),
        interpret=interpret,
    )(spectra, first, second, turn, cos_table, sin_table)


def on_device(signal, pair_band, pair_offset, pair_owner):
    channels = signal.shape[0]
    stride_count = BANDS // HOP
    frames_dev = signal.shape[1] // HOP
    blocks = lax.axis_size("tm")
    bank_table = bank_matrix(BANDS)
    sample_tail = passed_along(signal[:, : BANDS - HOP], "tm", -1)
    records = jnp.concatenate([signal, sample_tail], axis=1)
    pieces = records.reshape(channels, frames_dev + stride_count - 1, HOP)
    framed = jnp.concatenate(
        [pieces[:, part_index : part_index + frames_dev, :] for part_index in range(stride_count)],
        axis=2,
    )
    spectra = jnp.einsum(
        "cmn,nk->ckm", framed, bank_table, preferred_element_type=jnp.float32
    ).astype(jnp.bfloat16)
    spectra = spectra.reshape(channels, 2, BANDS, frames_dev)

    local_tables = jnp.stack([pair_band[0], pair_offset[0]], axis=0)
    spread = jnp.broadcast_to(local_tables[None], (blocks,) + local_tables.shape)
    tables = lax.all_to_all(spread, "tm", split_axis=0, concat_axis=0, tiled=True)
    bands_all = tables[:, 0].transpose(1, 0, 2)
    offsets_all = tables[:, 1].transpose(1, 0, 2)
    pairs = bands_all.shape[2]
    band_first = bands_all.reshape(channels, blocks * pairs)
    offset = offsets_all.reshape(channels, blocks * pairs)
    moment = lax.axis_index("tm") * frames_dev + jnp.arange(frames_dev, dtype=jnp.int32)
    step = math.gcd(HOP * FRAMES // BANDS, KEEP // 2, FRAMES)
    levels = FRAMES // step
    cos_table, sin_table = turn_table(jnp.arange(levels, dtype=jnp.int32) * step, moment)
    shift_bins = (offset * (HOP * FRAMES // BANDS) - KEEP // 2) % FRAMES
    demod = demodulated(
        spectra, band_first, band_first + offset, shift_bins // step, cos_table, sin_table, blocks
    )
    arrived = lax.all_to_all(demod, "tm", split_axis=0, concat_axis=0, tiled=True)
    rows = channels * pairs
    cosine_table, sine_table = fourier_tables()
    dft_table = jnp.stack(
        [
            jnp.concatenate([cosine_table, -sine_table], axis=1),
            jnp.concatenate([sine_table, cosine_table], axis=1),
        ],
        axis=0,
    ).reshape(2, blocks, frames_dev, 2 * KEEP)
    correlation = jnp.einsum(
        "tpcqm,ptmf->cqf", arrived, dft_table, preferred_element_type=jnp.float32
    ).astype(jnp.bfloat16).reshape(rows, 2 * KEEP)

    owner = pair_owner[0, :, :, 0].reshape(-1)
    groups = lax.axis_size("chan")
    capacity = max(2, 3 * owner.shape[0] // groups)
    hits = (owner[:, None] == jnp.arange(groups, dtype=jnp.int32)[None, :]).astype(jnp.int32)
    rank = jnp.sum((jnp.cumsum(hits, axis=0) - 1) * hits, axis=1)
    slot = owner * capacity + rank
    placing = (jnp.arange(groups * capacity, dtype=jnp.int32)[:, None] == slot[None, :]).astype(
        jnp.bfloat16
    )
    outgoing = jnp.dot(placing, correlation, preferred_element_type=jnp.float32).astype(
        jnp.bfloat16
    )
    outgoing = outgoing.reshape(groups, capacity, 2 * KEEP)
    arrived = lax.all_to_all(outgoing, "chan", split_axis=0, concat_axis=0, tiled=True)
    return arrived.reshape(1, 1, groups, capacity, 2 * KEEP)


def solution(mesh):
    return jax.shard_map(
        on_device,
        mesh=mesh,
        in_specs=(
            P("chan", "tm"),
            P("tm", "chan", None),
            P("tm", "chan", None),
            P("tm", "chan", None, None),
        ),
        out_specs=P("tm", "chan", None, None, None),
        check_vma=False,
    )
```

```python
import math

import jax
import jax.numpy as jnp
from jax import lax
from jax.sharding import PartitionSpec as P
from jax.experimental import pallas as pl

BANDS = 256
HOP = 64
FRAMES = 2048
KEEP = 1024
DMAX = 8


def passed_along(array, axis, by):
    devices = lax.axis_size(axis)
    pairs = [(i, i + by) for i in range(devices) if 0 <= i + by < devices]
    return lax.ppermute(array, axis, pairs)


def bank_matrix(bands):
    index = jnp.arange(bands, dtype=jnp.int32)
    angle = (index[:, None] * index[None, :] % bands).astype(jnp.float32) * (2.0 * math.pi / bands)
    window = 0.5 - 0.5 * jnp.cos((index.astype(jnp.float32) + 0.5) * (2.0 * math.pi / bands))
    scaled = window / math.sqrt(3.0 * bands / 8.0)
    return jnp.concatenate(
        [scaled[:, None] * jnp.cos(angle), -scaled[:, None] * jnp.sin(angle)], axis=1
    ).astype(jnp.bfloat16)


def turn_table(moments, cycles):
    angle = (moments[:, None] * cycles[None, :] % FRAMES).astype(jnp.float32) * (
        2.0 * math.pi / FRAMES
    )
    return jnp.cos(angle), jnp.sin(angle)


def fourier_tables(frames_dev):
    devices = FRAMES // frames_dev
    fine = 32
    coarse_count = FRAMES // fine
    cycles = jnp.arange(KEEP, dtype=jnp.int32)
    coarse_cos, coarse_sin = turn_table(fine * jnp.arange(coarse_count, dtype=jnp.int32), cycles)
    fine_cos, fine_sin = turn_table(jnp.arange(fine, dtype=jnp.int32), cycles)
    outer = (devices, 1, coarse_count // devices, 1, KEEP)
    inner = (1, 2, 1, fine // 2, KEEP)
    coarse_cos = coarse_cos.reshape(outer)
    coarse_sin = coarse_sin.reshape(outer)
    fine_cos = fine_cos.reshape(fine // 2, 2, KEEP).transpose(1, 0, 2).reshape(inner)
    fine_sin = fine_sin.reshape(fine // 2, 2, KEEP).transpose(1, 0, 2).reshape(inner)
    scale = 1.0 / math.sqrt(FRAMES)
    cosine = (coarse_cos * fine_cos - coarse_sin * fine_sin) * scale
    sine = (coarse_sin * fine_cos + coarse_cos * fine_sin) * scale
    return (
        cosine.reshape(FRAMES, KEEP).astype(jnp.bfloat16),
        sine.reshape(FRAMES, KEEP).astype(jnp.bfloat16),
    )


def demod_kernel(spec_ref, first_ref, second_ref, turn_ref, cos_ref, sin_ref, out_ref):
    per_block = spec_ref.shape[0]
    bands = spec_ref.shape[2]
    frames = spec_ref.shape[3]
    rows = first_ref.shape[1]
    blocks = out_ref.shape[0]
    pairs = out_ref.shape[3]
    positions = lax.broadcasted_iota(jnp.int32, (rows, bands), 1)
    first_all = first_ref[...].T
    second_all = second_ref[...].T
    turn_all = turn_ref[...].T
    for index in range(per_block):
        spectra = jnp.concatenate([spec_ref[index, 0], spec_ref[index, 1]], axis=1)
        pick = jnp.concatenate(
            [
                (first_all[:, index : index + 1] == positions).astype(jnp.bfloat16),
                (second_all[:, index : index + 1] == positions).astype(jnp.bfloat16),
            ],
            axis=0,
        )
        picked = jnp.dot(pick, spectra, preferred_element_type=jnp.float32)
        a_re = picked[:rows, :frames]
        a_im = picked[:rows, frames:]
        b_re = picked[rows:, :frames]
        b_im = picked[rows:, frames:]
        real_part = a_re * b_re + a_im * b_im
        imag_part = a_im * b_re - a_re * b_im
        turn = turn_all[:, index : index + 1]
        cosine = jnp.broadcast_to(cos_ref[0:1, :], (rows, frames))
        sine = jnp.broadcast_to(sin_ref[0:1, :], (rows, frames))
        for level in range(1, cos_ref.shape[0]):
            chosen = turn == level
            cosine = jnp.where(chosen, cos_ref[level : level + 1, :], cosine)
            sine = jnp.where(chosen, sin_ref[level : level + 1, :], sine)
        demod_re = (real_part * cosine + imag_part * sine).astype(out_ref.dtype)
        demod_im = (imag_part * cosine - real_part * sine).astype(out_ref.dtype)
        for block in range(blocks):
            out_ref[block, 0, index] = demod_re[block * pairs : (block + 1) * pairs]
            out_ref[block, 1, index] = demod_im[block * pairs : (block + 1) * pairs]


def demodulated(spectra, first, second, turn, cos_table, sin_table, blocks, per_block=8, interpret=False):
    channels, parts, bands, frames = spectra.shape
    rows = first.shape[1]
    pairs = rows // blocks
    levels = cos_table.shape[0]
    return pl.pallas_call(
        demod_kernel,
        out_shape=jax.ShapeDtypeStruct((blocks, 2, channels, pairs, frames), jnp.bfloat16),
        grid=(channels // per_block,),
        in_specs=[
            pl.BlockSpec((per_block, parts, bands, frames), lambda i: (i, 0, 0, 0)),
            pl.BlockSpec((per_block, rows), lambda i: (i, 0)),
            pl.BlockSpec((per_block, rows), lambda i: (i, 0)),
            pl.BlockSpec((per_block, rows), lambda i: (i, 0)),
            pl.BlockSpec((levels, frames), lambda i: (0, 0)),
            pl.BlockSpec((levels, frames), lambda i: (0, 0)),
        ],
        out_specs=pl.BlockSpec((blocks, 2, per_block, pairs, frames), lambda i: (0, 0, i, 0, 0)),
        interpret=interpret,
    )(spectra, first, second, turn, cos_table, sin_table)


def on_device(signal, pair_band, pair_offset, pair_owner):
    channels = signal.shape[0]
    stride_count = BANDS // HOP
    frames_dev = signal.shape[1] // HOP
    blocks = lax.axis_size("tm")
    bank_table = bank_matrix(BANDS)
    sample_tail = passed_along(signal[:, : BANDS - HOP], "tm", -1)
    half = frames_dev // 2
    span = 2 * HOP
    row_count = half + BANDS // span
    records = jnp.concatenate(
        [signal, sample_tail, jnp.zeros((channels, row_count * span - signal.shape[1] - BANDS + HOP), signal.dtype)],
        axis=1,
    ).reshape(channels, row_count, span)
    even_windows = jnp.concatenate(
        [records[:, j : j + half] for j in range(BANDS // span)], axis=2
    )
    odd_windows = jnp.concatenate(
        [records[:, j : j + half] for j in range(BANDS // span + 1)], axis=2
    )
    edge = jnp.zeros((HOP, 2 * BANDS), bank_table.dtype)
    odd_bank = jnp.concatenate([edge, bank_table, edge], axis=0)
    even_spectra = jnp.einsum(
        "cin,nk->cki", even_windows, bank_table, preferred_element_type=jnp.float32
    ).astype(jnp.bfloat16)
    odd_spectra = jnp.einsum(
        "cin,nk->cki", odd_windows, odd_bank, preferred_element_type=jnp.float32
    ).astype(jnp.bfloat16)
    spectra = jnp.concatenate([even_spectra, odd_spectra], axis=2)
    spectra = spectra.reshape(channels, 2, BANDS, frames_dev)

    local_tables = jnp.stack([pair_band[0], pair_offset[0]], axis=0)
    spread = jnp.broadcast_to(local_tables[None], (blocks,) + local_tables.shape)
    tables = lax.all_to_all(spread, "tm", split_axis=0, concat_axis=0, tiled=True)
    bands_all = tables[:, 0].transpose(1, 0, 2)
    offsets_all = tables[:, 1].transpose(1, 0, 2)
    pairs = bands_all.shape[2]
    band_first = bands_all.reshape(channels, blocks * pairs)
    offset = offsets_all.reshape(channels, blocks * pairs)
    local = jnp.arange(frames_dev, dtype=jnp.int32)
    moment = lax.axis_index("tm") * frames_dev + 2 * (local % half) + local // half
    step = math.gcd(HOP * FRAMES // BANDS, KEEP // 2, FRAMES)
    levels = FRAMES // step
    cos_table, sin_table = turn_table(jnp.arange(levels, dtype=jnp.int32) * step, moment)
    shift_bins = (offset * (HOP * FRAMES // BANDS) - KEEP // 2) % FRAMES
    demod = demodulated(
        spectra, band_first, band_first + offset, shift_bins // step, cos_table, sin_table, blocks
    )
    arrived = lax.all_to_all(demod, "tm", split_axis=0, concat_axis=0, tiled=True)
    arrived = arrived.transpose(1, 2, 3, 0, 4)
    rows = channels * pairs
    arrived = arrived.reshape(2 * rows, blocks * frames_dev)

    cosine_table, sine_table = fourier_tables(frames_dev)
    with_cos = jnp.dot(arrived, cosine_table, preferred_element_type=jnp.float32)
    with_sin = jnp.dot(arrived, sine_table, preferred_element_type=jnp.float32)
    corr_re = with_cos[:rows] + with_sin[rows:]
    corr_im = with_cos[rows:] - with_sin[:rows]
    correlation = jnp.concatenate([corr_re, corr_im], axis=1).astype(jnp.bfloat16)

    owner = pair_owner[0, :, :, 0].reshape(-1)
    groups = lax.axis_size("chan")
    capacity = max(2, 3 * owner.shape[0] // groups)
    hits = (owner[:, None] == jnp.arange(groups, dtype=jnp.int32)[None, :]).astype(jnp.int32)
    rank = jnp.sum((jnp.cumsum(hits, axis=0) - 1) * hits, axis=1)
    slot = owner * capacity + rank
    placing = (jnp.arange(groups * capacity, dtype=jnp.int32)[:, None] == slot[None, :]).astype(
        jnp.bfloat16
    )
    outgoing = jnp.dot(placing, correlation, preferred_element_type=jnp.float32).astype(
        jnp.bfloat16
    )
    outgoing = outgoing.reshape(groups, capacity, 2 * KEEP)
    arrived = lax.all_to_all(outgoing, "chan", split_axis=0, concat_axis=0, tiled=True)
    return arrived.reshape(1, 1, groups, capacity, 2 * KEEP)


def solution(mesh):
    return jax.shard_map(
        on_device,
        mesh=mesh,
        in_specs=(
            P("chan", "tm"),
            P("tm", "chan", None),
            P("tm", "chan", None),
            P("tm", "chan", None, None),
        ),
        out_specs=P("tm", "chan", None, None, None),
        check_vma=False,
    )
```

```python
import math

import jax
import numpy as np
import jax.numpy as jnp
from jax import lax
from jax.sharding import PartitionSpec as P
from jax.experimental import pallas as pl

BANDS = 256
HOP = 64
FRAMES = 2048
KEEP = 1024
DMAX = 8


def passed_along(array, axis, by):
    devices = lax.axis_size(axis)
    pairs = [(i, i + by) for i in range(devices) if 0 <= i + by < devices]
    return lax.ppermute(array, axis, pairs)


def bank_matrix(bands):
    index = np.arange(bands, dtype=np.int32)
    step = np.float32(2.0 * math.pi / bands)
    angle = (index[:, None] * index[None, :] % bands).astype(np.float32) * step
    window = np.float32(0.5) - np.float32(0.5) * np.cos((index.astype(np.float32) + np.float32(0.5)) * step)
    scaled = window / np.float32(math.sqrt(3.0 * bands / 8.0))
    table = np.concatenate(
        [scaled[:, None] * np.cos(angle), -scaled[:, None] * np.sin(angle)], axis=1
    ).astype(np.float32)
    return jnp.asarray(table, dtype=jnp.bfloat16)


def turn_table(moments, cycles):
    angle = (moments[:, None] * cycles[None, :] % FRAMES).astype(jnp.float32) * (
        2.0 * math.pi / FRAMES
    )
    return jnp.cos(angle), jnp.sin(angle)


def fourier_tables():
    cycles = jnp.arange(KEEP, dtype=jnp.int32)
    coarse_cos, coarse_sin = turn_table(32 * jnp.arange(FRAMES // 32, dtype=jnp.int32), cycles)
    fine_cos, fine_sin = turn_table(jnp.arange(32, dtype=jnp.int32), cycles)
    scale = 1.0 / math.sqrt(FRAMES)
    cosine = (
        coarse_cos[:, None, :] * fine_cos[None, :, :] - coarse_sin[:, None, :] * fine_sin[None, :, :]
    ) * scale
    sine = (
        coarse_sin[:, None, :] * fine_cos[None, :, :] + coarse_cos[:, None, :] * fine_sin[None, :, :]
    ) * scale
    return (
        cosine.reshape(FRAMES, KEEP).astype(jnp.bfloat16),
        sine.reshape(FRAMES, KEEP).astype(jnp.bfloat16),
    )


def demod_kernel(spec_ref, first_ref, second_ref, turn_ref, cos_ref, sin_ref, out_ref):
    per_block = spec_ref.shape[0]
    bands = spec_ref.shape[2]
    frames = spec_ref.shape[3]
    rows = first_ref.shape[1]
    blocks = out_ref.shape[0]
    pairs = out_ref.shape[3]
    positions = lax.broadcasted_iota(jnp.int32, (rows, bands), 1)
    first_all = first_ref[...].T
    second_all = second_ref[...].T
    turn_all = turn_ref[...].T
    for index in range(per_block):
        spectra = jnp.concatenate([spec_ref[index, 0], spec_ref[index, 1]], axis=1)
        pick = jnp.concatenate(
            [
                (first_all[:, index : index + 1] == positions).astype(jnp.bfloat16),
                (second_all[:, index : index + 1] == positions).astype(jnp.bfloat16),
            ],
            axis=0,
        )
        picked = jnp.dot(pick, spectra, preferred_element_type=jnp.float32)
        a_re = picked[:rows, :frames]
        a_im = picked[:rows, frames:]
        b_re = picked[rows:, :frames]
        b_im = picked[rows:, frames:]
        real_part = a_re * b_re + a_im * b_im
        imag_part = a_im * b_re - a_re * b_im
        turn = turn_all[:, index : index + 1]
        cosine = jnp.broadcast_to(cos_ref[0:1, :], (rows, frames))
        sine = jnp.broadcast_to(sin_ref[0:1, :], (rows, frames))
        for level in range(1, cos_ref.shape[0]):
            chosen = turn == level
            cosine = jnp.where(chosen, cos_ref[level : level + 1, :], cosine)
            sine = jnp.where(chosen, sin_ref[level : level + 1, :], sine)
        demod_re = (real_part * cosine + imag_part * sine).astype(out_ref.dtype)
        demod_im = (imag_part * cosine - real_part * sine).astype(out_ref.dtype)
        for block in range(blocks):
            out_ref[block, 0, index] = demod_re[block * pairs : (block + 1) * pairs]
            out_ref[block, 1, index] = demod_im[block * pairs : (block + 1) * pairs]


def demodulated(spectra, first, second, turn, cos_table, sin_table, blocks, per_block=8, interpret=False):
    channels, parts, bands, frames = spectra.shape
    rows = first.shape[1]
    pairs = rows // blocks
    levels = cos_table.shape[0]
    return pl.pallas_call(
        demod_kernel,
        out_shape=jax.ShapeDtypeStruct((blocks, 2, channels, pairs, frames), jnp.bfloat16),
        grid=(channels // per_block,),
        in_specs=[
            pl.BlockSpec((per_block, parts, bands, frames), lambda i: (i, 0, 0, 0)),
            pl.BlockSpec((per_block, rows), lambda i: (i, 0)),
            pl.BlockSpec((per_block, rows), lambda i: (i, 0)),
            pl.BlockSpec((per_block, rows), lambda i: (i, 0)),
            pl.BlockSpec((levels, frames), lambda i: (0, 0)),
            pl.BlockSpec((levels, frames), lambda i: (0, 0)),
        ],
        out_specs=pl.BlockSpec((blocks, 2, per_block, pairs, frames), lambda i: (0, 0, i, 0, 0)),
        interpret=interpret,
    )(spectra, first, second, turn, cos_table, sin_table)


def on_device(signal, pair_band, pair_offset, pair_owner):
    channels = signal.shape[0]
    stride_count = BANDS // HOP
    frames_dev = signal.shape[1] // HOP
    blocks = lax.axis_size("tm")
    bank_table = bank_matrix(BANDS)
    sample_tail = passed_along(signal[:, : BANDS - HOP], "tm", -1)
    records = jnp.concatenate([signal, sample_tail], axis=1)
    pieces = records.reshape(channels, frames_dev + stride_count - 1, HOP)
    framed = jnp.concatenate(
        [pieces[:, part_index : part_index + frames_dev, :] for part_index in range(stride_count)],
        axis=2,
    )
    spectra = jnp.einsum(
        "cmn,nk->ckm", framed, bank_table, preferred_element_type=jnp.float32
    ).astype(jnp.bfloat16)
    spectra = spectra.reshape(channels, 2, BANDS, frames_dev)

    local_tables = jnp.stack([pair_band[0], pair_offset[0]], axis=0)
    spread = jnp.broadcast_to(local_tables[None], (blocks,) + local_tables.shape)
    tables = lax.all_to_all(spread, "tm", split_axis=0, concat_axis=0, tiled=True)
    bands_all = tables[:, 0].transpose(1, 0, 2)
    offsets_all = tables[:, 1].transpose(1, 0, 2)
    pairs = bands_all.shape[2]
    band_first = bands_all.reshape(channels, blocks * pairs)
    offset = offsets_all.reshape(channels, blocks * pairs)
    moment = lax.axis_index("tm") * frames_dev + jnp.arange(frames_dev, dtype=jnp.int32)
    step = math.gcd(HOP * FRAMES // BANDS, KEEP // 2, FRAMES)
    levels = FRAMES // step
    cos_table, sin_table = turn_table(jnp.arange(levels, dtype=jnp.int32) * step, moment)
    shift_bins = (offset * (HOP * FRAMES // BANDS) - KEEP // 2) % FRAMES
    demod = demodulated(
        spectra, band_first, band_first + offset, shift_bins // step, cos_table, sin_table, blocks
    )
    arrived = lax.all_to_all(demod, "tm", split_axis=0, concat_axis=0, tiled=True)
    arrived = arrived.transpose(1, 2, 3, 0, 4)
    rows = channels * pairs
    arrived = arrived.reshape(2 * rows, blocks * frames_dev)

    cosine_table, sine_table = fourier_tables()
    with_cos = jnp.dot(arrived, cosine_table, preferred_element_type=jnp.float32)
    with_sin = jnp.dot(arrived, sine_table, preferred_element_type=jnp.float32)
    corr_re = with_cos[:rows] + with_sin[rows:]
    corr_im = with_cos[rows:] - with_sin[:rows]
    correlation = jnp.concatenate([corr_re, corr_im], axis=1).astype(jnp.bfloat16)

    owner = pair_owner[0, :, :, 0].reshape(-1)
    groups = lax.axis_size("chan")
    capacity = max(2, 3 * owner.shape[0] // groups)
    hits = (owner[:, None] == jnp.arange(groups, dtype=jnp.int32)[None, :]).astype(jnp.int32)
    rank = jnp.sum((jnp.cumsum(hits, axis=0) - 1) * hits, axis=1)
    slot = owner * capacity + rank
    placing = (jnp.arange(groups * capacity, dtype=jnp.int32)[:, None] == slot[None, :]).astype(
        jnp.bfloat16
    )
    outgoing = jnp.dot(placing, correlation, preferred_element_type=jnp.float32).astype(
        jnp.bfloat16
    )
    outgoing = outgoing.reshape(groups, capacity, 2 * KEEP)
    arrived = lax.all_to_all(outgoing, "chan", split_axis=0, concat_axis=0, tiled=True)
    return arrived.reshape(1, 1, groups, capacity, 2 * KEEP)


def solution(mesh):
    return jax.shard_map(
        on_device,
        mesh=mesh,
        in_specs=(
            P("chan", "tm"),
            P("tm", "chan", None),
            P("tm", "chan", None),
            P("tm", "chan", None, None),
        ),
        out_specs=P("tm", "chan", None, None, None),
        check_vma=False,
    )
```

```python
import math

import jax
import jax.numpy as jnp
from jax import lax
from jax.sharding import PartitionSpec as P
from jax.experimental import pallas as pl

BANDS = 256
HOP = 64
FRAMES = 2048
KEEP = 1024
DMAX = 8


def passed_along(array, axis, by):
    devices = lax.axis_size(axis)
    pairs = [(i, i + by) for i in range(devices) if 0 <= i + by < devices]
    return lax.ppermute(array, axis, pairs)


def bank_matrix(bands):
    index = jnp.arange(bands, dtype=jnp.int32)
    angle = (index[:, None] * index[None, :] % bands).astype(jnp.float32) * (2.0 * math.pi / bands)
    window = 0.5 - 0.5 * jnp.cos((index.astype(jnp.float32) + 0.5) * (2.0 * math.pi / bands))
    scaled = window / math.sqrt(3.0 * bands / 8.0)
    return jnp.concatenate(
        [scaled[:, None] * jnp.cos(angle), -scaled[:, None] * jnp.sin(angle)], axis=1
    ).astype(jnp.bfloat16)


def turn_table(moments, cycles):
    angle = (moments[:, None] * cycles[None, :] % FRAMES).astype(jnp.float32) * (
        2.0 * math.pi / FRAMES
    )
    return jnp.cos(angle), jnp.sin(angle)


def fourier_tables():
    cycles = jnp.arange(KEEP, dtype=jnp.int32)
    coarse_cos, coarse_sin = turn_table(32 * jnp.arange(FRAMES // 32, dtype=jnp.int32), cycles)
    fine_cos, fine_sin = turn_table(jnp.arange(32, dtype=jnp.int32), cycles)
    scale = 1.0 / math.sqrt(FRAMES)
    cosine = (
        coarse_cos[:, None, :] * fine_cos[None, :, :] - coarse_sin[:, None, :] * fine_sin[None, :, :]
    ) * scale
    sine = (
        coarse_sin[:, None, :] * fine_cos[None, :, :] + coarse_cos[:, None, :] * fine_sin[None, :, :]
    ) * scale
    return (
        cosine.reshape(FRAMES, KEEP).astype(jnp.bfloat16),
        sine.reshape(FRAMES, KEEP).astype(jnp.bfloat16),
    )


def demod_kernel(spec_ref, first_ref, second_ref, turn_ref, cos_ref, sin_ref, out_ref):
    per_block = spec_ref.shape[0]
    bands = spec_ref.shape[2]
    frames = spec_ref.shape[3]
    rows = first_ref.shape[1]
    blocks = out_ref.shape[0]
    pairs = out_ref.shape[3]
    positions = lax.broadcasted_iota(jnp.int32, (rows, bands), 1)
    first_all = first_ref[...].T
    second_all = second_ref[...].T
    turn_all = turn_ref[...].T
    for index in range(per_block):
        spectra = jnp.concatenate([spec_ref[index, 0], spec_ref[index, 1]], axis=1)
        pick = jnp.concatenate(
            [
                (first_all[:, index : index + 1] == positions).astype(jnp.bfloat16),
                (second_all[:, index : index + 1] == positions).astype(jnp.bfloat16),
            ],
            axis=0,
        )
        picked = jnp.dot(pick, spectra, preferred_element_type=jnp.float32)
        a_re = picked[:rows, :frames]
        a_im = picked[:rows, frames:]
        b_re = picked[rows:, :frames]
        b_im = picked[rows:, frames:]
        real_part = a_re * b_re + a_im * b_im
        imag_part = a_im * b_re - a_re * b_im
        turn = turn_all[:, index : index + 1]
        cosine = jnp.broadcast_to(cos_ref[0:1, :], (rows, frames))
        sine = jnp.broadcast_to(sin_ref[0:1, :], (rows, frames))
        for level in range(1, cos_ref.shape[0]):
            chosen = turn == level
            cosine = jnp.where(chosen, cos_ref[level : level + 1, :], cosine)
            sine = jnp.where(chosen, sin_ref[level : level + 1, :], sine)
        demod_re = (real_part * cosine + imag_part * sine).astype(out_ref.dtype)
        demod_im = (imag_part * cosine - real_part * sine).astype(out_ref.dtype)
        for block in range(blocks):
            out_ref[block, 0, index] = demod_re[block * pairs : (block + 1) * pairs]
            out_ref[block, 1, index] = demod_im[block * pairs : (block + 1) * pairs]


def demodulated(spectra, first, second, turn, cos_table, sin_table, blocks, per_block=8, interpret=False):
    channels, parts, bands, frames = spectra.shape
    rows = first.shape[1]
    pairs = rows // blocks
    levels = cos_table.shape[0]
    return pl.pallas_call(
        demod_kernel,
        out_shape=jax.ShapeDtypeStruct((blocks, 2, channels, pairs, frames), jnp.bfloat16),
        grid=(channels // per_block,),
        in_specs=[
            pl.BlockSpec((per_block, parts, bands, frames), lambda i: (i, 0, 0, 0)),
            pl.BlockSpec((per_block, rows), lambda i: (i, 0)),
            pl.BlockSpec((per_block, rows), lambda i: (i, 0)),
            pl.BlockSpec((per_block, rows), lambda i: (i, 0)),
            pl.BlockSpec((levels, frames), lambda i: (0, 0)),
            pl.BlockSpec((levels, frames), lambda i: (0, 0)),
        ],
        out_specs=pl.BlockSpec((blocks, 2, per_block, pairs, frames), lambda i: (0, 0, i, 0, 0)),
        interpret=interpret,
    )(spectra, first, second, turn, cos_table, sin_table)


def on_device(signal, pair_band, pair_offset, pair_owner):
    channels = signal.shape[0]
    stride_count = BANDS // HOP
    frames_dev = signal.shape[1] // HOP
    blocks = lax.axis_size("tm")
    bank_table = bank_matrix(BANDS)
    sample_tail = passed_along(signal[:, : BANDS - HOP], "tm", -1)
    records = jnp.concatenate([signal, sample_tail], axis=1)
    pieces = records.reshape(channels, frames_dev + stride_count - 1, HOP)
    framed = jnp.concatenate(
        [pieces[:, part_index : part_index + frames_dev, :] for part_index in range(stride_count)],
        axis=2,
    )
    spectra = jnp.einsum(
        "cmn,nk->ckm", framed, bank_table, preferred_element_type=jnp.float32
    ).astype(jnp.bfloat16)
    spectra = spectra.reshape(channels, 2, BANDS, frames_dev)

    local_tables = jnp.stack([pair_band[0], pair_offset[0]], axis=0)
    spread = jnp.broadcast_to(local_tables[None], (blocks,) + local_tables.shape)
    tables = lax.all_to_all(spread, "tm", split_axis=0, concat_axis=0, tiled=True)
    bands_all = tables[:, 0].transpose(1, 0, 2)
    offsets_all = tables[:, 1].transpose(1, 0, 2)
    pairs = bands_all.shape[2]
    band_first = bands_all.reshape(channels, blocks * pairs)
    offset = offsets_all.reshape(channels, blocks * pairs)
    moment = lax.axis_index("tm") * frames_dev + jnp.arange(frames_dev, dtype=jnp.int32)
    step = math.gcd(HOP * FRAMES // BANDS, KEEP // 2, FRAMES)
    levels = FRAMES // step
    cos_table, sin_table = turn_table(jnp.arange(levels, dtype=jnp.int32) * step, moment)
    shift_bins = (offset * (HOP * FRAMES // BANDS) - KEEP // 2) % FRAMES
    demod = demodulated(
        spectra, band_first, band_first + offset, shift_bins // step, cos_table, sin_table, blocks
    )
    arrived = lax.all_to_all(demod, "tm", split_axis=0, concat_axis=0, tiled=True)
    rows = channels * pairs
    cosine_table, sine_table = fourier_tables()
    both_tables = jnp.concatenate([cosine_table, sine_table], axis=1).reshape(
        blocks, frames_dev, 2 * KEEP
    )
    with_both = jnp.einsum(
        "tpcqm,tmf->pcqf", arrived, both_tables, preferred_element_type=jnp.float32
    ).reshape(2, rows, 2 * KEEP)
    corr_re = with_both[0, :, :KEEP] + with_both[1, :, KEEP:]
    corr_im = with_both[1, :, :KEEP] - with_both[0, :, KEEP:]
    correlation = jnp.concatenate([corr_re, corr_im], axis=1).astype(jnp.bfloat16)

    owner = pair_owner[0, :, :, 0].reshape(-1)
    groups = lax.axis_size("chan")
    capacity = max(2, 3 * owner.shape[0] // groups)
    hits = (owner[:, None] == jnp.arange(groups, dtype=jnp.int32)[None, :]).astype(jnp.int32)
    rank = jnp.sum((jnp.cumsum(hits, axis=0) - 1) * hits, axis=1)
    slot = owner * capacity + rank
    placing = (jnp.arange(groups * capacity, dtype=jnp.int32)[:, None] == slot[None, :]).astype(
        jnp.bfloat16
    )
    outgoing = jnp.dot(placing, correlation, preferred_element_type=jnp.float32).astype(
        jnp.bfloat16
    )
    outgoing = outgoing.reshape(groups, capacity, 2 * KEEP)
    arrived = lax.all_to_all(outgoing, "chan", split_axis=0, concat_axis=0, tiled=True)
    return arrived.reshape(1, 1, groups, capacity, 2 * KEEP)


def solution(mesh):
    return jax.shard_map(
        on_device,
        mesh=mesh,
        in_specs=(
            P("chan", "tm"),
            P("tm", "chan", None),
            P("tm", "chan", None),
            P("tm", "chan", None, None),
        ),
        out_specs=P("tm", "chan", None, None, None),
        check_vma=False,
    )
```

```python
import math

import jax
import jax.numpy as jnp
from jax import lax
from jax.sharding import PartitionSpec as P
from jax.experimental import pallas as pl

BANDS = 256
HOP = 64
FRAMES = 2048
KEEP = 1024
DMAX = 8


def passed_along(array, axis, by):
    devices = lax.axis_size(axis)
    pairs = [(i, i + by) for i in range(devices) if 0 <= i + by < devices]
    return lax.ppermute(array, axis, pairs)


def bank_matrix(bands):
    index = jnp.arange(bands, dtype=jnp.int32)
    angle = (index[:, None] * index[None, :] % bands).astype(jnp.float32) * (2.0 * math.pi / bands)
    window = 0.5 - 0.5 * jnp.cos((index.astype(jnp.float32) + 0.5) * (2.0 * math.pi / bands))
    scaled = window / math.sqrt(3.0 * bands / 8.0)
    return jnp.concatenate(
        [scaled[:, None] * jnp.cos(angle), -scaled[:, None] * jnp.sin(angle)], axis=1
    ).astype(jnp.bfloat16)


def turn_table(moments, cycles):
    angle = (moments[:, None] * cycles[None, :] % FRAMES).astype(jnp.float32) * (
        2.0 * math.pi / FRAMES
    )
    return jnp.cos(angle), jnp.sin(angle)


def fourier_tables():
    cycles = jnp.arange(KEEP, dtype=jnp.int32)
    coarse_cos, coarse_sin = turn_table(32 * jnp.arange(FRAMES // 32, dtype=jnp.int32), cycles)
    fine_cos, fine_sin = turn_table(jnp.arange(32, dtype=jnp.int32), cycles)
    scale = 1.0 / math.sqrt(FRAMES)
    cosine = (
        coarse_cos[:, None, :] * fine_cos[None, :, :] - coarse_sin[:, None, :] * fine_sin[None, :, :]
    ) * scale
    sine = (
        coarse_sin[:, None, :] * fine_cos[None, :, :] + coarse_cos[:, None, :] * fine_sin[None, :, :]
    ) * scale
    return (
        cosine.reshape(FRAMES, KEEP).astype(jnp.bfloat16),
        sine.reshape(FRAMES, KEEP).astype(jnp.bfloat16),
    )


def demod_kernel(spec_ref, first_ref, second_ref, turn_ref, cos_ref, sin_ref, out_ref):
    per_block = spec_ref.shape[0]
    bands = spec_ref.shape[2]
    frames = spec_ref.shape[3]
    rows = first_ref.shape[1]
    blocks = out_ref.shape[0]
    pairs = out_ref.shape[3]
    positions = lax.broadcasted_iota(jnp.int32, (rows, bands), 1)
    first_all = first_ref[...].T
    second_all = second_ref[...].T
    turn_all = turn_ref[...].T
    for index in range(per_block):
        spectra = jnp.concatenate([spec_ref[index, 0], spec_ref[index, 1]], axis=1)
        pick = jnp.concatenate(
            [
                (first_all[:, index : index + 1] == positions).astype(jnp.bfloat16),
                (second_all[:, index : index + 1] == positions).astype(jnp.bfloat16),
            ],
            axis=0,
        )
        picked = jnp.dot(pick, spectra, preferred_element_type=jnp.float32)
        a_re = picked[:rows, :frames]
        a_im = picked[:rows, frames:]
        b_re = picked[rows:, :frames]
        b_im = picked[rows:, frames:]
        real_part = a_re * b_re + a_im * b_im
        imag_part = a_im * b_re - a_re * b_im
        turn = turn_all[:, index : index + 1]
        cosine = jnp.broadcast_to(cos_ref[0:1, :], (rows, frames))
        sine = jnp.broadcast_to(sin_ref[0:1, :], (rows, frames))
        for level in range(1, cos_ref.shape[0]):
            chosen = turn == level
            cosine = jnp.where(chosen, cos_ref[level : level + 1, :], cosine)
            sine = jnp.where(chosen, sin_ref[level : level + 1, :], sine)
        demod_re = (real_part * cosine + imag_part * sine).astype(out_ref.dtype)
        demod_im = (imag_part * cosine - real_part * sine).astype(out_ref.dtype)
        for block in range(blocks):
            out_ref[block, 0, index] = demod_re[block * pairs : (block + 1) * pairs]
            out_ref[block, 1, index] = demod_im[block * pairs : (block + 1) * pairs]


def demodulated(spectra, first, second, turn, cos_table, sin_table, blocks, per_block=8, interpret=False):
    channels, parts, bands, frames = spectra.shape
    rows = first.shape[1]
    pairs = rows // blocks
    levels = cos_table.shape[0]
    return pl.pallas_call(
        demod_kernel,
        out_shape=jax.ShapeDtypeStruct((blocks, 2, channels, pairs, frames), jnp.bfloat16),
        grid=(channels // per_block,),
        in_specs=[
            pl.BlockSpec((per_block, parts, bands, frames), lambda i: (i, 0, 0, 0)),
            pl.BlockSpec((per_block, rows), lambda i: (i, 0)),
            pl.BlockSpec((per_block, rows), lambda i: (i, 0)),
            pl.BlockSpec((per_block, rows), lambda i: (i, 0)),
            pl.BlockSpec((levels, frames), lambda i: (0, 0)),
            pl.BlockSpec((levels, frames), lambda i: (0, 0)),
        ],
        out_specs=pl.BlockSpec((blocks, 2, per_block, pairs, frames), lambda i: (0, 0, i, 0, 0)),
        interpret=interpret,
    )(spectra, first, second, turn, cos_table, sin_table)


def on_device(signal, pair_band, pair_offset, pair_owner):
    channels = signal.shape[0]
    stride_count = BANDS // HOP
    frames_dev = signal.shape[1] // HOP
    blocks = lax.axis_size("tm")
    bank_table = bank_matrix(BANDS)
    sample_tail = passed_along(signal[:, : BANDS - HOP], "tm", -1)
    records = jnp.concatenate([signal, sample_tail], axis=1)
    pieces = records.reshape(channels, frames_dev + stride_count - 1, HOP)
    framed = jnp.concatenate(
        [pieces[:, part_index : part_index + frames_dev, :] for part_index in range(stride_count)],
        axis=2,
    )
    spectra = jnp.einsum(
        "cmn,nk->ckm", framed, bank_table, preferred_element_type=jnp.float32
    ).astype(jnp.bfloat16)
    spectra = spectra.reshape(channels, 2, BANDS, frames_dev)

    local_tables = jnp.stack([pair_band[0], pair_offset[0]], axis=0)
    spread = jnp.broadcast_to(local_tables[None], (blocks,) + local_tables.shape)
    tables = lax.all_to_all(spread, "tm", split_axis=0, concat_axis=0, tiled=True)
    bands_all = tables[:, 0].transpose(1, 0, 2)
    offsets_all = tables[:, 1].transpose(1, 0, 2)
    pairs = bands_all.shape[2]
    band_first = bands_all.reshape(channels, blocks * pairs)
    offset = offsets_all.reshape(channels, blocks * pairs)
    moment = lax.axis_index("tm") * frames_dev + jnp.arange(frames_dev, dtype=jnp.int32)
    step = math.gcd(HOP * FRAMES // BANDS, KEEP // 2, FRAMES)
    levels = FRAMES // step
    cos_table, sin_table = turn_table(jnp.arange(levels, dtype=jnp.int32) * step, moment)
    shift_bins = (offset * (HOP * FRAMES // BANDS) - KEEP // 2) % FRAMES
    demod = demodulated(
        spectra, band_first, band_first + offset, shift_bins // step, cos_table, sin_table, blocks
    )
    arrived = lax.all_to_all(demod, "tm", split_axis=0, concat_axis=0, tiled=True)
    rows = channels * pairs
    cosine_table, sine_table = fourier_tables()
    dft_table = jnp.stack(
        [
            jnp.concatenate([cosine_table, -sine_table], axis=1),
            jnp.concatenate([sine_table, cosine_table], axis=1),
        ],
        axis=0,
    ).reshape(2, blocks, frames_dev, 2 * KEEP)
    dft_table = lax.optimization_barrier(dft_table)
    correlation = jnp.einsum(
        "tpcqm,ptmf->cqf", arrived, dft_table, preferred_element_type=jnp.float32
    ).astype(jnp.bfloat16).reshape(rows, 2 * KEEP)


    owner = pair_owner[0, :, :, 0].reshape(-1)
    groups = lax.axis_size("chan")
    capacity = max(2, 3 * owner.shape[0] // groups)
    hits = (owner[:, None] == jnp.arange(groups, dtype=jnp.int32)[None, :]).astype(jnp.int32)
    rank = jnp.sum((jnp.cumsum(hits, axis=0) - 1) * hits, axis=1)
    slot = owner * capacity + rank
    placing = (jnp.arange(groups * capacity, dtype=jnp.int32)[:, None] == slot[None, :]).astype(
        jnp.bfloat16
    )
    outgoing = jnp.dot(placing, correlation, preferred_element_type=jnp.float32).astype(
        jnp.bfloat16
    )
    outgoing = outgoing.reshape(groups, capacity, 2 * KEEP)
    arrived = lax.all_to_all(outgoing, "chan", split_axis=0, concat_axis=0, tiled=True)
    return arrived.reshape(1, 1, groups, capacity, 2 * KEEP)


def solution(mesh):
    return jax.shard_map(
        on_device,
        mesh=mesh,
        in_specs=(
            P("chan", "tm"),
            P("tm", "chan", None),
            P("tm", "chan", None),
            P("tm", "chan", None, None),
        ),
        out_specs=P("tm", "chan", None, None, None),
        check_vma=False,
    )
```

```python
import math

import jax
import jax.numpy as jnp
from jax import lax
from jax.sharding import PartitionSpec as P
from jax.experimental import pallas as pl

BANDS = 256
HOP = 64
FRAMES = 2048
KEEP = 1024
DMAX = 8


def passed_along(array, axis, by):
    devices = lax.axis_size(axis)
    pairs = [(i, i + by) for i in range(devices) if 0 <= i + by < devices]
    return lax.ppermute(array, axis, pairs)


def bank_matrix(bands):
    index = jnp.arange(bands, dtype=jnp.int32)
    angle = (index[:, None] * index[None, :] % bands).astype(jnp.float32) * (2.0 * math.pi / bands)
    window = 0.5 - 0.5 * jnp.cos((index.astype(jnp.float32) + 0.5) * (2.0 * math.pi / bands))
    scaled = window / math.sqrt(3.0 * bands / 8.0)
    return jnp.concatenate(
        [scaled[:, None] * jnp.cos(angle), -scaled[:, None] * jnp.sin(angle)], axis=1
    ).astype(jnp.bfloat16)


def turn_table(moments, cycles):
    angle = (moments[:, None] * cycles[None, :] % FRAMES).astype(jnp.float32) * (
        2.0 * math.pi / FRAMES
    )
    return jnp.cos(angle), jnp.sin(angle)


def fourier_tables():
    cycles = jnp.arange(KEEP, dtype=jnp.int32)
    coarse_cos, coarse_sin = turn_table(32 * jnp.arange(FRAMES // 32, dtype=jnp.int32), cycles)
    fine_cos, fine_sin = turn_table(jnp.arange(32, dtype=jnp.int32), cycles)
    scale = 1.0 / math.sqrt(FRAMES)
    cosine = (
        coarse_cos[:, None, :] * fine_cos[None, :, :] - coarse_sin[:, None, :] * fine_sin[None, :, :]
    ) * scale
    sine = (
        coarse_sin[:, None, :] * fine_cos[None, :, :] + coarse_cos[:, None, :] * fine_sin[None, :, :]
    ) * scale
    return (
        cosine.reshape(FRAMES, KEEP).astype(jnp.bfloat16),
        sine.reshape(FRAMES, KEEP).astype(jnp.bfloat16),
    )


def demod_kernel(spec_ref, first_ref, second_ref, turn_ref, cos_ref, sin_ref, out_ref):
    per_block = spec_ref.shape[0]
    bands = spec_ref.shape[2]
    frames = spec_ref.shape[3]
    rows = first_ref.shape[1]
    blocks = out_ref.shape[0]
    pairs = out_ref.shape[3]
    positions = lax.broadcasted_iota(jnp.int32, (rows, bands), 1)
    first_all = first_ref[...].T
    second_all = second_ref[...].T
    turn_all = turn_ref[...].T
    for index in range(per_block):
        spectra = jnp.concatenate([spec_ref[index, 0], spec_ref[index, 1]], axis=1)
        pick = jnp.concatenate(
            [
                (first_all[:, index : index + 1] == positions).astype(jnp.bfloat16),
                (second_all[:, index : index + 1] == positions).astype(jnp.bfloat16),
            ],
            axis=0,
        )
        picked = jnp.dot(pick, spectra, preferred_element_type=jnp.float32)
        a_re = picked[:rows, :frames]
        a_im = picked[:rows, frames:]
        b_re = picked[rows:, :frames]
        b_im = picked[rows:, frames:]
        real_part = a_re * b_re + a_im * b_im
        imag_part = a_im * b_re - a_re * b_im
        turn = turn_all[:, index : index + 1]
        cosine = jnp.broadcast_to(cos_ref[0:1, :], (rows, frames))
        sine = jnp.broadcast_to(sin_ref[0:1, :], (rows, frames))
        for level in range(1, cos_ref.shape[0]):
            chosen = turn == level
            cosine = jnp.where(chosen, cos_ref[level : level + 1, :], cosine)
            sine = jnp.where(chosen, sin_ref[level : level + 1, :], sine)
        demod_re = (real_part * cosine + imag_part * sine).astype(out_ref.dtype)
        demod_im = (imag_part * cosine - real_part * sine).astype(out_ref.dtype)
        for block in range(blocks):
            out_ref[block, 0, index] = demod_re[block * pairs : (block + 1) * pairs]
            out_ref[block, 1, index] = demod_im[block * pairs : (block + 1) * pairs]


def demodulated(spectra, first, second, turn, cos_table, sin_table, blocks, per_block=8, interpret=False):
    channels, parts, bands, frames = spectra.shape
    rows = first.shape[1]
    pairs = rows // blocks
    levels = cos_table.shape[0]
    return pl.pallas_call(
        demod_kernel,
        out_shape=jax.ShapeDtypeStruct((blocks, 2, channels, pairs, frames), jnp.bfloat16),
        grid=(channels // per_block,),
        in_specs=[
            pl.BlockSpec((per_block, parts, bands, frames), lambda i: (i, 0, 0, 0)),
            pl.BlockSpec((per_block, rows), lambda i: (i, 0)),
            pl.BlockSpec((per_block, rows), lambda i: (i, 0)),
            pl.BlockSpec((per_block, rows), lambda i: (i, 0)),
            pl.BlockSpec((levels, frames), lambda i: (0, 0)),
            pl.BlockSpec((levels, frames), lambda i: (0, 0)),
        ],
        out_specs=pl.BlockSpec((blocks, 2, per_block, pairs, frames), lambda i: (0, 0, i, 0, 0)),
        interpret=interpret,
    )(spectra, first, second, turn, cos_table, sin_table)


def on_device(signal, pair_band, pair_offset, pair_owner):
    channels = signal.shape[0]
    stride_count = BANDS // HOP
    frames_dev = signal.shape[1] // HOP
    blocks = lax.axis_size("tm")
    bank_table = bank_matrix(BANDS)
    sample_tail = passed_along(signal[:, : BANDS - HOP], "tm", -1)
    records = jnp.concatenate([signal, sample_tail], axis=1)
    pieces = records.reshape(channels, frames_dev + stride_count - 1, HOP)
    framed = jnp.concatenate(
        [pieces[:, part_index : part_index + frames_dev, :] for part_index in range(stride_count)],
        axis=2,
    )
    spectra = jnp.einsum(
        "cmn,nk->ckm", framed, bank_table, preferred_element_type=jnp.float32
    ).astype(jnp.bfloat16)
    spectra = spectra.reshape(channels, 2, BANDS, frames_dev)

    step = math.gcd(HOP * FRAMES // BANDS, KEEP // 2, FRAMES)
    levels = FRAMES // step
    band = pair_band[0]
    shift_bins = (pair_offset[0] * (HOP * FRAMES // BANDS) - KEEP // 2) % FRAMES
    local_tables = jnp.stack([band, band + pair_offset[0], shift_bins // step], axis=0)
    pairs = band.shape[1]
    spread = jnp.broadcast_to(
        local_tables[:, :, None, :], (3, channels, blocks, pairs)
    )
    tables = lax.all_to_all(spread, "tm", split_axis=2, concat_axis=2, tiled=True)
    tables = tables.reshape(3, channels, blocks * pairs)
    moment = lax.axis_index("tm") * frames_dev + jnp.arange(frames_dev, dtype=jnp.int32)
    cos_table, sin_table = turn_table(jnp.arange(levels, dtype=jnp.int32) * step, moment)
    demod = demodulated(
        spectra, tables[0], tables[1], tables[2], cos_table, sin_table, blocks
    )
    arrived = lax.all_to_all(demod, "tm", split_axis=0, concat_axis=0, tiled=True)
    rows = channels * pairs
    cosine_table, sine_table = fourier_tables()
    both_tables = jnp.concatenate([cosine_table, sine_table], axis=1).reshape(
        blocks, frames_dev, 2 * KEEP
    )
    with_both = jnp.einsum(
        "tpcqm,tmf->pcqf", arrived, both_tables, preferred_element_type=jnp.float32
    ).reshape(2, rows, 2 * KEEP)
    corr_re = with_both[0, :, :KEEP] + with_both[1, :, KEEP:]
    corr_im = with_both[1, :, :KEEP] - with_both[0, :, KEEP:]
    correlation = jnp.concatenate([corr_re, corr_im], axis=1).astype(jnp.bfloat16)

    owner = pair_owner[0, :, :, 0].reshape(-1)
    groups = lax.axis_size("chan")
    capacity = max(2, 3 * owner.shape[0] // groups)
    hits = (owner[:, None] == jnp.arange(groups, dtype=jnp.int32)[None, :]).astype(jnp.int32)
    rank = jnp.sum((jnp.cumsum(hits, axis=0) - 1) * hits, axis=1)
    slot = owner * capacity + rank
    placing = (jnp.arange(groups * capacity, dtype=jnp.int32)[:, None] == slot[None, :]).astype(
        jnp.bfloat16
    )
    outgoing = jnp.dot(placing, correlation, preferred_element_type=jnp.float32).astype(
        jnp.bfloat16
    )
    outgoing = outgoing.reshape(groups, capacity, 2 * KEEP)
    arrived = lax.all_to_all(outgoing, "chan", split_axis=0, concat_axis=0, tiled=True)
    return arrived.reshape(1, 1, groups, capacity, 2 * KEEP)


def solution(mesh):
    return jax.shard_map(
        on_device,
        mesh=mesh,
        in_specs=(
            P("chan", "tm"),
            P("tm", "chan", None),
            P("tm", "chan", None),
            P("tm", "chan", None, None),
        ),
        out_specs=P("tm", "chan", None, None, None),
        check_vma=False,
    )
```

```python
import math

import jax
import jax.numpy as jnp
from jax import lax
from jax.sharding import PartitionSpec as P
from jax.experimental import pallas as pl

BANDS = 256
HOP = 64
FRAMES = 2048
KEEP = 1024
DMAX = 8


def passed_along(array, axis, by):
    devices = lax.axis_size(axis)
    pairs = [(i, i + by) for i in range(devices) if 0 <= i + by < devices]
    return lax.ppermute(array, axis, pairs)


def bank_matrix(bands):
    index = jnp.arange(bands, dtype=jnp.int32)
    angle = (index[:, None] * index[None, :] % bands).astype(jnp.float32) * (2.0 * math.pi / bands)
    window = 0.5 - 0.5 * jnp.cos((index.astype(jnp.float32) + 0.5) * (2.0 * math.pi / bands))
    scaled = window / math.sqrt(3.0 * bands / 8.0)
    return jnp.concatenate(
        [scaled[:, None] * jnp.cos(angle), -scaled[:, None] * jnp.sin(angle)], axis=1
    ).astype(jnp.bfloat16)


def turn_table(moments, cycles):
    angle = (moments[:, None] * cycles[None, :] % FRAMES).astype(jnp.float32) * (
        2.0 * math.pi / FRAMES
    )
    return jnp.cos(angle), jnp.sin(angle)


def fourier_tables():
    cycles = jnp.arange(KEEP, dtype=jnp.int32)
    coarse_cos, coarse_sin = turn_table(32 * jnp.arange(FRAMES // 32, dtype=jnp.int32), cycles)
    fine_cos, fine_sin = turn_table(jnp.arange(32, dtype=jnp.int32), cycles)
    scale = 1.0 / math.sqrt(FRAMES)
    cosine = (
        coarse_cos[:, None, :] * fine_cos[None, :, :] - coarse_sin[:, None, :] * fine_sin[None, :, :]
    ) * scale
    sine = (
        coarse_sin[:, None, :] * fine_cos[None, :, :] + coarse_cos[:, None, :] * fine_sin[None, :, :]
    ) * scale
    return (
        cosine.reshape(FRAMES, KEEP).astype(jnp.bfloat16),
        sine.reshape(FRAMES, KEEP).astype(jnp.bfloat16),
    )


def demod_kernel(spec_ref, first_ref, second_ref, turn_ref, cos_ref, sin_ref, out_ref):
    per_block = spec_ref.shape[0]
    bands = spec_ref.shape[2]
    frames = spec_ref.shape[3]
    rows = first_ref.shape[1]
    blocks = out_ref.shape[0]
    pairs = out_ref.shape[3]
    positions = lax.broadcasted_iota(jnp.int32, (rows, bands), 1)
    first_all = first_ref[...].T
    second_all = second_ref[...].T
    turn_all = turn_ref[...].T
    for index in range(per_block):
        spectra = jnp.concatenate([spec_ref[index, 0], spec_ref[index, 1]], axis=1)
        pick = jnp.concatenate(
            [
                (first_all[:, index : index + 1] == positions).astype(jnp.bfloat16),
                (second_all[:, index : index + 1] == positions).astype(jnp.bfloat16),
            ],
            axis=0,
        )
        picked = jnp.dot(pick, spectra, preferred_element_type=jnp.float32)
        a_re = picked[:rows, :frames]
        a_im = picked[:rows, frames:]
        b_re = picked[rows:, :frames]
        b_im = picked[rows:, frames:]
        real_part = a_re * b_re + a_im * b_im
        imag_part = a_im * b_re - a_re * b_im
        turn = turn_all[:, index : index + 1]
        cosine = jnp.broadcast_to(cos_ref[0:1, :], (rows, frames))
        sine = jnp.broadcast_to(sin_ref[0:1, :], (rows, frames))
        for level in range(1, cos_ref.shape[0]):
            chosen = turn == level
            cosine = jnp.where(chosen, cos_ref[level : level + 1, :], cosine)
            sine = jnp.where(chosen, sin_ref[level : level + 1, :], sine)
        demod_re = real_part * cosine + imag_part * sine
        demod_im = imag_part * cosine - real_part * sine
        for block in range(blocks):
            rows_of = slice(block * pairs, (block + 1) * pairs)
            out_ref[block, 0, index] = demod_re[rows_of].astype(out_ref.dtype)
            out_ref[block, 1, index] = demod_im[rows_of].astype(out_ref.dtype)


def demodulated(spectra, first, second, turn, cos_table, sin_table, blocks, per_block=8, interpret=False):
    channels, parts, bands, frames = spectra.shape
    rows = first.shape[1]
    pairs = rows // blocks
    levels = cos_table.shape[0]
    return pl.pallas_call(
        demod_kernel,
        out_shape=jax.ShapeDtypeStruct((blocks, 2, channels, pairs, frames), jnp.bfloat16),
        grid=(channels // per_block,),
        in_specs=[
            pl.BlockSpec((per_block, parts, bands, frames), lambda i: (i, 0, 0, 0)),
            pl.BlockSpec((per_block, rows), lambda i: (i, 0)),
            pl.BlockSpec((per_block, rows), lambda i: (i, 0)),
            pl.BlockSpec((per_block, rows), lambda i: (i, 0)),
            pl.BlockSpec((levels, frames), lambda i: (0, 0)),
            pl.BlockSpec((levels, frames), lambda i: (0, 0)),
        ],
        out_specs=pl.BlockSpec((blocks, 2, per_block, pairs, frames), lambda i: (0, 0, i, 0, 0)),
        interpret=interpret,
    )(spectra, first, second, turn, cos_table, sin_table)


def on_device(signal, pair_band, pair_offset, pair_owner):
    channels = signal.shape[0]
    stride_count = BANDS // HOP
    frames_dev = signal.shape[1] // HOP
    blocks = lax.axis_size("tm")
    bank_table = bank_matrix(BANDS)
    sample_tail = passed_along(signal[:, : BANDS - HOP], "tm", -1)
    records = jnp.concatenate([signal, sample_tail], axis=1)
    pieces = records.reshape(channels, frames_dev + stride_count - 1, HOP)
    framed = jnp.concatenate(
        [pieces[:, part_index : part_index + frames_dev, :] for part_index in range(stride_count)],
        axis=2,
    )
    spectra = jnp.einsum(
        "cmn,nk->ckm", framed, bank_table, preferred_element_type=jnp.float32
    ).astype(jnp.bfloat16)
    spectra = spectra.reshape(channels, 2, BANDS, frames_dev)

    local_tables = jnp.stack([pair_band[0], pair_offset[0]], axis=0)
    spread = jnp.broadcast_to(local_tables[None], (blocks,) + local_tables.shape)
    tables = lax.all_to_all(spread, "tm", split_axis=0, concat_axis=0, tiled=True)
    bands_all = tables[:, 0].transpose(1, 0, 2)
    offsets_all = tables[:, 1].transpose(1, 0, 2)
    pairs = bands_all.shape[2]
    band_first = bands_all.reshape(channels, blocks * pairs)
    offset = offsets_all.reshape(channels, blocks * pairs)
    moment = lax.axis_index("tm") * frames_dev + jnp.arange(frames_dev, dtype=jnp.int32)
    step = math.gcd(HOP * FRAMES // BANDS, KEEP // 2, FRAMES)
    levels = FRAMES // step
    cos_table, sin_table = turn_table(jnp.arange(levels, dtype=jnp.int32) * step, moment)
    shift_bins = (offset * (HOP * FRAMES // BANDS) - KEEP // 2) % FRAMES
    demod = demodulated(
        spectra, band_first, band_first + offset, shift_bins // step, cos_table, sin_table, blocks
    )
    arrived = lax.all_to_all(demod, "tm", split_axis=0, concat_axis=0, tiled=True)
    rows = channels * pairs
    cosine_table, sine_table = fourier_tables()
    both_tables = jnp.concatenate([cosine_table, sine_table], axis=1).reshape(
        blocks, frames_dev, 2 * KEEP
    )
    with_both = jnp.einsum(
        "tpcqm,tmf->pcqf", arrived, both_tables, preferred_element_type=jnp.float32
    ).reshape(2, rows, 2 * KEEP)
    corr_re = with_both[0, :, :KEEP] + with_both[1, :, KEEP:]
    corr_im = with_both[1, :, :KEEP] - with_both[0, :, KEEP:]
    correlation = jnp.concatenate([corr_re, corr_im], axis=1).astype(jnp.bfloat16)

    owner = pair_owner[0, :, :, 0].reshape(-1)
    groups = lax.axis_size("chan")
    capacity = max(2, 3 * owner.shape[0] // groups)
    hits = (owner[:, None] == jnp.arange(groups, dtype=jnp.int32)[None, :]).astype(jnp.int32)
    rank = jnp.sum((jnp.cumsum(hits, axis=0) - 1) * hits, axis=1)
    slot = owner * capacity + rank
    placing = (jnp.arange(groups * capacity, dtype=jnp.int32)[:, None] == slot[None, :]).astype(
        jnp.bfloat16
    )
    outgoing = jnp.dot(placing, correlation, preferred_element_type=jnp.float32).astype(
        jnp.bfloat16
    )
    outgoing = outgoing.reshape(groups, capacity, 2 * KEEP)
    arrived = lax.all_to_all(outgoing, "chan", split_axis=0, concat_axis=0, tiled=True)
    return arrived.reshape(1, 1, groups, capacity, 2 * KEEP)


def solution(mesh):
    return jax.shard_map(
        on_device,
        mesh=mesh,
        in_specs=(
            P("chan", "tm"),
            P("tm", "chan", None),
            P("tm", "chan", None),
            P("tm", "chan", None, None),
        ),
        out_specs=P("tm", "chan", None, None, None),
        check_vma=False,
    )
```

```python
import math

import jax
import jax.numpy as jnp
from jax import lax
from jax.sharding import PartitionSpec as P
from jax.experimental import pallas as pl

BANDS = 256
HOP = 64
FRAMES = 2048
KEEP = 1024
DMAX = 8


def passed_along(array, axis, by):
    devices = lax.axis_size(axis)
    pairs = [(i, i + by) for i in range(devices) if 0 <= i + by < devices]
    return lax.ppermute(array, axis, pairs)


def bank_matrix(bands):
    index = jnp.arange(bands, dtype=jnp.int32)
    angle = (index[:, None] * index[None, :] % bands).astype(jnp.float32) * (2.0 * math.pi / bands)
    window = 0.5 - 0.5 * jnp.cos((index.astype(jnp.float32) + 0.5) * (2.0 * math.pi / bands))
    scaled = window / math.sqrt(3.0 * bands / 8.0)
    return jnp.concatenate(
        [scaled[:, None] * jnp.cos(angle), -scaled[:, None] * jnp.sin(angle)], axis=1
    ).astype(jnp.bfloat16)


def turn_table(moments, cycles):
    angle = (moments[:, None] * cycles[None, :] % FRAMES).astype(jnp.float32) * (
        2.0 * math.pi / FRAMES
    )
    return jnp.cos(angle), jnp.sin(angle)


def fourier_tables():
    cycles = jnp.arange(KEEP, dtype=jnp.int32)
    coarse_cos, coarse_sin = turn_table(32 * jnp.arange(FRAMES // 32, dtype=jnp.int32), cycles)
    fine_cos, fine_sin = turn_table(jnp.arange(32, dtype=jnp.int32), cycles)
    scale = 1.0 / math.sqrt(FRAMES)
    cosine = (
        coarse_cos[:, None, :] * fine_cos[None, :, :] - coarse_sin[:, None, :] * fine_sin[None, :, :]
    ) * scale
    sine = (
        coarse_sin[:, None, :] * fine_cos[None, :, :] + coarse_cos[:, None, :] * fine_sin[None, :, :]
    ) * scale
    return (
        cosine.reshape(FRAMES, KEEP).astype(jnp.bfloat16),
        sine.reshape(FRAMES, KEEP).astype(jnp.bfloat16),
    )


def demod_kernel(spec_ref, first_ref, second_ref, turn_ref, cos_ref, sin_ref, out_ref):
    per_block = spec_ref.shape[0]
    bands = spec_ref.shape[2]
    frames = spec_ref.shape[3]
    rows = first_ref.shape[1]
    blocks = out_ref.shape[0]
    pairs = out_ref.shape[3]
    positions = lax.broadcasted_iota(jnp.int32, (rows, bands), 1)
    first_all = first_ref[...].T
    second_all = second_ref[...].T
    turn_all = turn_ref[...].T
    for index in range(per_block):
        spec_re = spec_ref[index, 0]
        spec_im = spec_ref[index, 1]
        pick_a = (first_all[:, index : index + 1] == positions).astype(jnp.bfloat16)
        pick_b = (second_all[:, index : index + 1] == positions).astype(jnp.bfloat16)
        a_re = jnp.dot(pick_a, spec_re, preferred_element_type=jnp.float32)
        a_im = jnp.dot(pick_a, spec_im, preferred_element_type=jnp.float32)
        b_re = jnp.dot(pick_b, spec_re, preferred_element_type=jnp.float32)
        b_im = jnp.dot(pick_b, spec_im, preferred_element_type=jnp.float32)
        real_part = a_re * b_re + a_im * b_im
        imag_part = a_im * b_re - a_re * b_im
        turn = turn_all[:, index : index + 1]
        cosine = jnp.broadcast_to(cos_ref[0:1, :], (rows, frames))
        sine = jnp.broadcast_to(sin_ref[0:1, :], (rows, frames))
        for level in range(1, cos_ref.shape[0]):
            chosen = turn == level
            cosine = jnp.where(chosen, cos_ref[level : level + 1, :], cosine)
            sine = jnp.where(chosen, sin_ref[level : level + 1, :], sine)
        demod_re = (real_part * cosine + imag_part * sine).astype(out_ref.dtype)
        demod_im = (imag_part * cosine - real_part * sine).astype(out_ref.dtype)
        for block in range(blocks):
            out_ref[block, 0, index] = demod_re[block * pairs : (block + 1) * pairs]
            out_ref[block, 1, index] = demod_im[block * pairs : (block + 1) * pairs]


def demodulated(spectra, first, second, turn, cos_table, sin_table, blocks, per_block=8, interpret=False):
    channels, parts, bands, frames = spectra.shape
    rows = first.shape[1]
    pairs = rows // blocks
    levels = cos_table.shape[0]
    return pl.pallas_call(
        demod_kernel,
        out_shape=jax.ShapeDtypeStruct((blocks, 2, channels, pairs, frames), jnp.bfloat16),
        grid=(channels // per_block,),
        in_specs=[
            pl.BlockSpec((per_block, parts, bands, frames), lambda i: (i, 0, 0, 0)),
            pl.BlockSpec((per_block, rows), lambda i: (i, 0)),
            pl.BlockSpec((per_block, rows), lambda i: (i, 0)),
            pl.BlockSpec((per_block, rows), lambda i: (i, 0)),
            pl.BlockSpec((levels, frames), lambda i: (0, 0)),
            pl.BlockSpec((levels, frames), lambda i: (0, 0)),
        ],
        out_specs=pl.BlockSpec((blocks, 2, per_block, pairs, frames), lambda i: (0, 0, i, 0, 0)),
        interpret=interpret,
    )(spectra, first, second, turn, cos_table, sin_table)


def on_device(signal, pair_band, pair_offset, pair_owner):
    channels = signal.shape[0]
    stride_count = BANDS // HOP
    frames_dev = signal.shape[1] // HOP
    blocks = lax.axis_size("tm")
    bank_table = bank_matrix(BANDS)
    sample_tail = passed_along(signal[:, : BANDS - HOP], "tm", -1)
    records = jnp.concatenate([signal, sample_tail], axis=1)
    pieces = records.reshape(channels, frames_dev + stride_count - 1, HOP)
    framed = jnp.concatenate(
        [pieces[:, part_index : part_index + frames_dev, :] for part_index in range(stride_count)],
        axis=2,
    )
    spectra = jnp.einsum(
        "cmn,nk->ckm", framed, bank_table, preferred_element_type=jnp.float32
    ).astype(jnp.bfloat16)
    spectra = spectra.reshape(channels, 2, BANDS, frames_dev)

    local_tables = jnp.stack([pair_band[0], pair_offset[0]], axis=0)
    spread = jnp.broadcast_to(local_tables[None], (blocks,) + local_tables.shape)
    tables = lax.all_to_all(spread, "tm", split_axis=0, concat_axis=0, tiled=True)
    bands_all = tables[:, 0].transpose(1, 0, 2)
    offsets_all = tables[:, 1].transpose(1, 0, 2)
    pairs = bands_all.shape[2]
    band_first = bands_all.reshape(channels, blocks * pairs)
    offset = offsets_all.reshape(channels, blocks * pairs)
    moment = lax.axis_index("tm") * frames_dev + jnp.arange(frames_dev, dtype=jnp.int32)
    step = math.gcd(HOP * FRAMES // BANDS, KEEP // 2, FRAMES)
    levels = FRAMES // step
    cos_table, sin_table = turn_table(jnp.arange(levels, dtype=jnp.int32) * step, moment)
    shift_bins = (offset * (HOP * FRAMES // BANDS) - KEEP // 2) % FRAMES
    demod = demodulated(
        spectra, band_first, band_first + offset, shift_bins // step, cos_table, sin_table, blocks
    )
    arrived = lax.all_to_all(demod, "tm", split_axis=0, concat_axis=0, tiled=True)
    rows = channels * pairs
    cosine_table, sine_table = fourier_tables()
    both_tables = jnp.concatenate([cosine_table, sine_table], axis=1).reshape(
        blocks, frames_dev, 2 * KEEP
    )
    with_both = jnp.einsum(
        "tpcqm,tmf->pcqf", arrived, both_tables, preferred_element_type=jnp.float32
    ).reshape(2, rows, 2 * KEEP)
    corr_re = with_both[0, :, :KEEP] + with_both[1, :, KEEP:]
    corr_im = with_both[1, :, :KEEP] - with_both[0, :, KEEP:]
    correlation = jnp.concatenate([corr_re, corr_im], axis=1).astype(jnp.bfloat16)

    owner = pair_owner[0, :, :, 0].reshape(-1)
    groups = lax.axis_size("chan")
    capacity = max(2, 3 * owner.shape[0] // groups)
    hits = (owner[:, None] == jnp.arange(groups, dtype=jnp.int32)[None, :]).astype(jnp.int32)
    rank = jnp.sum((jnp.cumsum(hits, axis=0) - 1) * hits, axis=1)
    slot = owner * capacity + rank
    placing = (jnp.arange(groups * capacity, dtype=jnp.int32)[:, None] == slot[None, :]).astype(
        jnp.bfloat16
    )
    outgoing = jnp.dot(placing, correlation, preferred_element_type=jnp.float32).astype(
        jnp.bfloat16
    )
    outgoing = outgoing.reshape(groups, capacity, 2 * KEEP)
    arrived = lax.all_to_all(outgoing, "chan", split_axis=0, concat_axis=0, tiled=True)
    return arrived.reshape(1, 1, groups, capacity, 2 * KEEP)


def solution(mesh):
    return jax.shard_map(
        on_device,
        mesh=mesh,
        in_specs=(
            P("chan", "tm"),
            P("tm", "chan", None),
            P("tm", "chan", None),
            P("tm", "chan", None, None),
        ),
        out_specs=P("tm", "chan", None, None, None),
        check_vma=False,
    )
```

```python
import math

import jax
import jax.numpy as jnp
from jax import lax
from jax.sharding import PartitionSpec as P
from jax.experimental import pallas as pl

BANDS = 256
HOP = 64
FRAMES = 2048
KEEP = 1024
DMAX = 8


def passed_along(array, axis, by):
    devices = lax.axis_size(axis)
    pairs = [(i, i + by) for i in range(devices) if 0 <= i + by < devices]
    return lax.ppermute(array, axis, pairs)


def bank_matrix(bands):
    index = jnp.arange(bands, dtype=jnp.int32)
    angle = (index[:, None] * index[None, :] % bands).astype(jnp.float32) * (2.0 * math.pi / bands)
    window = 0.5 - 0.5 * jnp.cos((index.astype(jnp.float32) + 0.5) * (2.0 * math.pi / bands))
    scaled = window / math.sqrt(3.0 * bands / 8.0)
    return jnp.concatenate(
        [scaled[:, None] * jnp.cos(angle), -scaled[:, None] * jnp.sin(angle)], axis=1
    ).astype(jnp.bfloat16)


def turn_table(moments, cycles):
    angle = (moments[:, None] * cycles[None, :] % FRAMES).astype(jnp.float32) * (
        2.0 * math.pi / FRAMES
    )
    return jnp.cos(angle), jnp.sin(angle)


def fourier_tables():
    cycles = jnp.arange(KEEP, dtype=jnp.int32)
    coarse_cos, coarse_sin = turn_table(32 * jnp.arange(FRAMES // 32, dtype=jnp.int32), cycles)
    fine_cos, fine_sin = turn_table(jnp.arange(32, dtype=jnp.int32), cycles)
    scale = 1.0 / math.sqrt(FRAMES)
    cosine = (
        coarse_cos[:, None, :] * fine_cos[None, :, :] - coarse_sin[:, None, :] * fine_sin[None, :, :]
    ) * scale
    sine = (
        coarse_sin[:, None, :] * fine_cos[None, :, :] + coarse_cos[:, None, :] * fine_sin[None, :, :]
    ) * scale
    return (
        cosine.reshape(FRAMES, KEEP).astype(jnp.bfloat16),
        sine.reshape(FRAMES, KEEP).astype(jnp.bfloat16),
    )


def demod_kernel(spec_ref, first_ref, second_ref, turn_ref, cos_ref, sin_ref, out_ref):
    per_block = spec_ref.shape[0]
    bands = spec_ref.shape[2]
    frames = spec_ref.shape[3]
    rows = first_ref.shape[1]
    blocks = out_ref.shape[0]
    pairs = out_ref.shape[3]
    positions = lax.broadcasted_iota(jnp.int32, (rows, bands), 1)
    first_all = first_ref[...].T
    second_all = second_ref[...].T
    turn_all = turn_ref[...].T
    for index in range(per_block):
        spectra = jnp.concatenate([spec_ref[index, 0], spec_ref[index, 1]], axis=1)
        pick = jnp.concatenate(
            [
                (first_all[:, index : index + 1] == positions).astype(jnp.bfloat16),
                (second_all[:, index : index + 1] == positions).astype(jnp.bfloat16),
            ],
            axis=0,
        )
        picked = jnp.dot(pick, spectra, preferred_element_type=jnp.float32)
        a_re = picked[:rows, :frames]
        a_im = picked[:rows, frames:]
        b_re = picked[rows:, :frames]
        b_im = picked[rows:, frames:]
        real_part = a_re * b_re + a_im * b_im
        imag_part = a_im * b_re - a_re * b_im
        turn = turn_all[:, index : index + 1]
        cosine = jnp.broadcast_to(cos_ref[0:1, :], (rows, frames))
        sine = jnp.broadcast_to(sin_ref[0:1, :], (rows, frames))
        for level in range(1, cos_ref.shape[0]):
            chosen = turn == level
            cosine = jnp.where(chosen, cos_ref[level : level + 1, :], cosine)
            sine = jnp.where(chosen, sin_ref[level : level + 1, :], sine)
        demod_re = (real_part * cosine + imag_part * sine).astype(out_ref.dtype)
        demod_im = (imag_part * cosine - real_part * sine).astype(out_ref.dtype)
        for block in range(blocks):
            out_ref[block, 0, index] = demod_re[block * pairs : (block + 1) * pairs]
            out_ref[block, 1, index] = demod_im[block * pairs : (block + 1) * pairs]


def demodulated(spectra, first, second, turn, cos_table, sin_table, blocks, per_block=16, interpret=False):
    channels, parts, bands, frames = spectra.shape
    rows = first.shape[1]
    pairs = rows // blocks
    levels = cos_table.shape[0]
    return pl.pallas_call(
        demod_kernel,
        out_shape=jax.ShapeDtypeStruct((blocks, 2, channels, pairs, frames), jnp.bfloat16),
        grid=(channels // per_block,),
        in_specs=[
            pl.BlockSpec((per_block, parts, bands, frames), lambda i: (i, 0, 0, 0)),
            pl.BlockSpec((per_block, rows), lambda i: (i, 0)),
            pl.BlockSpec((per_block, rows), lambda i: (i, 0)),
            pl.BlockSpec((per_block, rows), lambda i: (i, 0)),
            pl.BlockSpec((levels, frames), lambda i: (0, 0)),
            pl.BlockSpec((levels, frames), lambda i: (0, 0)),
        ],
        out_specs=pl.BlockSpec((blocks, 2, per_block, pairs, frames), lambda i: (0, 0, i, 0, 0)),
        interpret=interpret,
    )(spectra, first, second, turn, cos_table, sin_table)


def on_device(signal, pair_band, pair_offset, pair_owner):
    channels = signal.shape[0]
    stride_count = BANDS // HOP
    frames_dev = signal.shape[1] // HOP
    blocks = lax.axis_size("tm")
    bank_table = bank_matrix(BANDS)
    sample_tail = passed_along(signal[:, : BANDS - HOP], "tm", -1)
    records = jnp.concatenate([signal, sample_tail], axis=1)
    pieces = records.reshape(channels, frames_dev + stride_count - 1, HOP)
    framed = jnp.concatenate(
        [pieces[:, part_index : part_index + frames_dev, :] for part_index in range(stride_count)],
        axis=2,
    )
    spectra = jnp.einsum(
        "cmn,nk->ckm", framed, bank_table, preferred_element_type=jnp.float32
    ).astype(jnp.bfloat16)
    spectra = spectra.reshape(channels, 2, BANDS, frames_dev)

    local_tables = jnp.stack([pair_band[0], pair_offset[0]], axis=0)
    spread = jnp.broadcast_to(local_tables[None], (blocks,) + local_tables.shape)
    tables = lax.all_to_all(spread, "tm", split_axis=0, concat_axis=0, tiled=True)
    bands_all = tables[:, 0].transpose(1, 0, 2)
    offsets_all = tables[:, 1].transpose(1, 0, 2)
    pairs = bands_all.shape[2]
    band_first = bands_all.reshape(channels, blocks * pairs)
    offset = offsets_all.reshape(channels, blocks * pairs)
    moment = lax.axis_index("tm") * frames_dev + jnp.arange(frames_dev, dtype=jnp.int32)
    step = math.gcd(HOP * FRAMES // BANDS, KEEP // 2, FRAMES)
    levels = FRAMES // step
    cos_table, sin_table = turn_table(jnp.arange(levels, dtype=jnp.int32) * step, moment)
    shift_bins = (offset * (HOP * FRAMES // BANDS) - KEEP // 2) % FRAMES
    demod = demodulated(
        spectra, band_first, band_first + offset, shift_bins // step, cos_table, sin_table, blocks
    )
    arrived = lax.all_to_all(demod, "tm", split_axis=0, concat_axis=0, tiled=True)
    rows = channels * pairs
    cosine_table, sine_table = fourier_tables()
    both_tables = jnp.concatenate([cosine_table, sine_table], axis=1).reshape(
        blocks, frames_dev, 2 * KEEP
    )
    with_both = jnp.einsum(
        "tpcqm,tmf->pcqf", arrived, both_tables, preferred_element_type=jnp.float32
    ).reshape(2, rows, 2 * KEEP)
    corr_re = with_both[0, :, :KEEP] + with_both[1, :, KEEP:]
    corr_im = with_both[1, :, :KEEP] - with_both[0, :, KEEP:]
    correlation = jnp.concatenate([corr_re, corr_im], axis=1).astype(jnp.bfloat16)

    owner = pair_owner[0, :, :, 0].reshape(-1)
    groups = lax.axis_size("chan")
    capacity = max(2, 3 * owner.shape[0] // groups)
    hits = (owner[:, None] == jnp.arange(groups, dtype=jnp.int32)[None, :]).astype(jnp.int32)
    rank = jnp.sum((jnp.cumsum(hits, axis=0) - 1) * hits, axis=1)
    slot = owner * capacity + rank
    placing = (jnp.arange(groups * capacity, dtype=jnp.int32)[:, None] == slot[None, :]).astype(
        jnp.bfloat16
    )
    outgoing = jnp.dot(placing, correlation, preferred_element_type=jnp.float32).astype(
        jnp.bfloat16
    )
    outgoing = outgoing.reshape(groups, capacity, 2 * KEEP)
    arrived = lax.all_to_all(outgoing, "chan", split_axis=0, concat_axis=0, tiled=True)
    return arrived.reshape(1, 1, groups, capacity, 2 * KEEP)


def solution(mesh):
    return jax.shard_map(
        on_device,
        mesh=mesh,
        in_specs=(
            P("chan", "tm"),
            P("tm", "chan", None),
            P("tm", "chan", None),
            P("tm", "chan", None, None),
        ),
        out_specs=P("tm", "chan", None, None, None),
        check_vma=False,
    )
```
